512 devices in a mesh: band: 16 (over x, y), lon: 32 (over z, core).
Axes of the slice: x: 4, y: 4, z: 16, core: 2. Of those that a mesh axis runs over, the one named last changes fastest.
Arguments:
- sky_maps: float32 [16, 8192, 256], P(None, ('band', 'lon')), may hold values from -9 to 9
- noise_var: float32 [8192, 256], P(('band', 'lon')), may hold values from 1 to 4
- position: float32 [3, 8192, 256], P(None, ('band', 'lon')), may hold values from -1 to 1
- leaf_basis: float32 [8192, 256, 64], P(('band', 'lon')), may hold values from -1 to 1
- leaf_couple: float32 [8192, 4, 64, 64], P(('band', 'lon')), as said below
- transfer: float32 [8192, 64, 64], P(('band', 'lon')), may hold values from -2 to 2
- panel_couple: float32 [1024, 2, 64, 64], P(('band', 'lon')), as said below
- near_list: int32 [8192, 5], P(('band', 'lon')), may hold values from -1 to 8191, as said below
- far_list: int32 [8192, 4], P(('band', 'lon')), may hold values from 0 to 8191, as said below
- panel_list: int32 [1024, 2], P(('band', 'lon')), may hold values from 0 to 1023, as said below
- leaf_panel: int32 [8192], P(('band', 'lon')), may hold values from 0 to 1
Outputs:
- solution: float32 [16, 8192, 256], P(None, ('band', 'lon'))
- residual: float32 [16, 8192, 256], P(None, ('band', 'lon'))
The draws below stay inside these ranges and needn't reach their ends.
Inputs may be any that keep to these rules, and one draw needn't show every extreme that they name: `near_list`: entry 0 of a row is the leaf itself; the entries after it that are not -1 come first and are distinct leaves of the same band at cycle distance 1 or 2, the cycle closing; leaf j stands in leaf i's row exactly when i stands in j's. `far_list`: distinct leaves of the same band at cycle distance 3 to 6, the cycle closing; leaf j stands in leaf i's row exactly when i stands in j's. If leaf j stands in slot s of far_list[i] and leaf i in slot t of far_list[j], then leaf_couple[j, t] is the transpose of leaf_couple[i, s]. `panel_list`: entries are panel s of sectors of other bands at the same longitude (sector ids differing by a nonzero multiple of the sectors of a band), s being the panel's own index in its sector; panel j stands in panel k's row as often as k stands in j's. If panel j stands in slot s of panel_list[k] and these slots pair up with the slots t of panel_list[j] that hold k, then panel_couple[j, t] is the transpose of panel_couple[k, s].
All inputs are finite; a program needn't handle non-finite values.
Results may differ from the reference program's by a relative error of at most 0.0003.
Values sent between devices are 32-bit elements; how exact they have to be, the bound alone decides.
No kernel may reach another device: no remote copies, remote signals or barrier semaphores. Data moves between devices by JAX's collectives and lax.ppermute only.
A program may use at most 128 MiB of HBM per device.

```python
import math
import jax
import jax.numpy as jnp
from jax import lax

P_SIZE = 256
R = 64
NEAR = 5
FAR1 = 4
FAR2 = 2
REACH = 6
ITERS = 2
PANEL_DEV = 2
LEAF_DEV = 16
MAPS = 16
CYCLE = 512
LEAVES = 8192
PANELS = 1024


COMMON_PART = 0.5


def corner_mask(rank):
    first_row = jnp.arange(rank)[:, None] == 0
    first_col = jnp.arange(rank)[None, :] == 0
    return jnp.logical_and(first_row, first_col).astype(jnp.float32)


def draw_sky_maps(key, part):
    sector_frac = (jnp.arange(LEAVES) // LEAF_DEV).astype(jnp.float32) / (LEAVES // LEAF_DEV - 1)
    spread = 0.5 * jnp.power(3.0, sector_frac)
    raw_vals = jax.random.truncated_normal(key, -5.0, 5.0, (MAPS, LEAVES, P_SIZE)) + 0.5
    return (raw_vals * spread[None, :, None]).astype(jnp.float32)


def draw_leaf_basis(key, part):
    shape = (LEAVES, P_SIZE, R)
    raw_vals = jax.random.truncated_normal(key, -6.0, 6.0, shape)
    column_shift = jnp.where(jnp.arange(R) == 0, COMMON_PART, 0.0).astype(jnp.float32)
    return ((raw_vals + column_shift[None, None, :]) * P_SIZE ** (-0.5)).astype(jnp.float32)


def draw_transfer(key, part):
    shape = (LEAVES, R, R)
    raw_vals = jax.random.truncated_normal(key, -6.0, 6.0, shape)
    fan_in = R * LEAF_DEV // PANEL_DEV
    return (raw_vals * fan_in ** (-0.5) + COMMON_PART * corner_mask(R)[None]).astype(jnp.float32)


def draw_position(key, part):
    band_count = LEAVES // CYCLE
    leaf_ids = jnp.arange(LEAVES)
    band_of = (leaf_ids // CYCLE).astype(jnp.float32)
    cycle_pos = (leaf_ids % CYCLE).astype(jnp.float32)
    leaf_width = 2.0 * jnp.pi / CYCLE
    center_lat = -1.1 + 2.2 * (band_of + 0.5) / band_count
    center_lon = leaf_width * (cycle_pos + 0.5)
    along_frac = jax.random.uniform(jax.random.fold_in(key, 41), (LEAVES, P_SIZE))
    across_frac = jax.random.uniform(jax.random.fold_in(key, 42), (LEAVES, P_SIZE))
    lon_vals = center_lon[:, None] + leaf_width * (along_frac - 0.5)
    lat_vals = center_lat[:, None] + leaf_width * jnp.cos(center_lat)[:, None] * (across_frac - 0.5)
    return jnp.stack([jnp.cos(lat_vals) * jnp.cos(lon_vals), jnp.cos(lat_vals) * jnp.sin(lon_vals), jnp.sin(lat_vals)], axis=0).astype(jnp.float32)


def draw_near_list(key, part):
    band_count = LEAVES // CYCLE
    leaf_ids = jnp.arange(LEAVES, dtype=jnp.int32)
    band_of = leaf_ids // CYCLE
    cycle_pos = leaf_ids % CYCLE
    polar_band = (jnp.abs(2 * band_of + 1 - band_count) * 2 >= band_count).astype(jnp.int32)
    cutoff = 3 + 6 * polar_band
    edge_one = (jax.random.randint(jax.random.fold_in(key, 31), (LEAVES,), 0, 10) < cutoff).astype(jnp.int32)
    edge_two = (jax.random.randint(jax.random.fold_in(key, 32), (LEAVES,), 0, 10) < cutoff).astype(jnp.int32)
    back_two = band_of * CYCLE + (cycle_pos - 2) % CYCLE
    back_one = band_of * CYCLE + (cycle_pos - 1) % CYCLE
    ahead_one = band_of * CYCLE + (cycle_pos + 1) % CYCLE
    ahead_two = band_of * CYCLE + (cycle_pos + 2) % CYCLE
    cand_ids = jnp.stack([back_two, back_one, ahead_one, ahead_two], axis=1)
    cand_live = jnp.stack([edge_two[back_two], edge_one[back_one], edge_one, edge_two], axis=1)
    leaf_keys = jax.random.split(jax.random.fold_in(key, 33), LEAVES)
    shuffle = jax.vmap(lambda sub_key: jax.random.permutation(sub_key, jnp.arange(4, dtype=jnp.int32)))(leaf_keys)
    cand_ids = jnp.take_along_axis(cand_ids, shuffle, axis=1)
    cand_live = jnp.take_along_axis(cand_live, shuffle, axis=1)
    ranking = jnp.argsort(1 - cand_live, axis=1, stable=True)
    cand_ids = jnp.take_along_axis(cand_ids, ranking, axis=1)
    cand_live = jnp.take_along_axis(cand_live, ranking, axis=1)
    others = jnp.where(cand_live == 1, cand_ids, -1)
    return jnp.concatenate([leaf_ids[:, None], others], axis=1).astype(jnp.int32)


def far_slots(key):
    band_count = LEAVES // CYCLE
    band_of = jnp.arange(LEAVES, dtype=jnp.int32) // CYCLE
    band_keys = jax.random.split(jax.random.fold_in(key, 11), band_count)
    picked = jax.vmap(lambda sub_key: jax.random.permutation(sub_key, jnp.arange(3, REACH + 1, dtype=jnp.int32)))(band_keys)
    picked = picked[:, :FAR1 // 2]
    signed = jnp.concatenate([picked, -picked], axis=1)[band_of]
    leaf_keys = jax.random.split(jax.random.fold_in(key, 12), LEAVES)
    return jax.vmap(lambda sub_key, row_vals: jax.random.permutation(sub_key, row_vals))(leaf_keys, signed)


def far_partners(offsets):
    leaf_ids = jnp.arange(LEAVES, dtype=jnp.int32)
    return (leaf_ids // CYCLE)[:, None] * CYCLE + ((leaf_ids % CYCLE)[:, None] + offsets) % CYCLE


def draw_far_list(key, part):
    return far_partners(far_slots(key)).astype(jnp.int32)


def draw_leaf_couple(key, part):
    offsets = far_slots(key)
    partner = far_partners(offsets)
    leaf_ids = jnp.arange(LEAVES, dtype=jnp.int32)
    shape = (LEAVES, REACH - 2, R, R)
    forward = jax.random.normal(jax.random.fold_in(key, 13), shape)
    forward = forward * (R * FAR1) ** (-0.5)
    source = jnp.where(offsets > 0, leaf_ids[:, None], partner)
    edge_slot = jnp.abs(offsets) - 3
    chosen = forward[source, edge_slot]
    flipped = jnp.swapaxes(chosen, 2, 3)
    return jnp.where((offsets > 0)[:, :, None, None], chosen, flipped).astype(jnp.float32)


def panel_slots(key):
    band_count = LEAVES // CYCLE
    sectors = CYCLE // LEAF_DEV
    panel_ids = jnp.arange(PANELS, dtype=jnp.int32)
    column = panel_ids // PANEL_DEV % sectors
    band_steps = jax.random.randint(jax.random.fold_in(key, 21), (sectors,), 1, band_count // 2 + 1)[column]
    swap_flag = jax.random.randint(jax.random.fold_in(key, 22), (PANELS,), 0, 2)
    first_step = jnp.where(swap_flag == 1, -band_steps, band_steps)
    return jnp.stack([first_step, -first_step], axis=1)


def panel_partners(offsets):
    band_count = LEAVES // CYCLE
    band_panels = PANEL_DEV * (CYCLE // LEAF_DEV)
    panel_ids = jnp.arange(PANELS, dtype=jnp.int32)
    band_of = panel_ids // band_panels
    within = panel_ids % band_panels
    return (band_of[:, None] + offsets) % band_count * band_panels + within[:, None]


def draw_panel_list(key, part):
    return panel_partners(panel_slots(key)).astype(jnp.int32)


def draw_panel_couple(key, part):
    offsets = panel_slots(key)
    partner = panel_partners(offsets)
    panel_ids = jnp.arange(PANELS, dtype=jnp.int32)
    shape = (PANELS, R, R)
    forward = jax.random.normal(jax.random.fold_in(key, 23), shape)
    forward = forward * (R * FAR2) ** (-0.5) + COMMON_PART * corner_mask(R)[None]
    source = jnp.where(offsets > 0, panel_ids[:, None], partner)
    chosen = forward[source]
    flipped = jnp.swapaxes(chosen, 2, 3)
    return jnp.where((offsets > 0)[:, :, None, None], chosen, flipped).astype(jnp.float32)


def plant(entries, stream_key, least, top_value):
    longest = entries.shape.index(max(entries.shape))
    spots = []
    for shift in (0, 1):
        where = [jax.random.randint(jax.random.fold_in(stream_key, axis), (), 0, length) for axis, length in enumerate(entries.shape)]
        where[longest] = (where[longest] + shift) % entries.shape[longest]
        spots.append(tuple(where))
    return entries.at[spots[0]].set(least).at[spots[1]].set(top_value)


def steps_of(own_key, dims, shards, smallest, largest):
    gain = 1.0
    for axis_at, blocks in shards:
        heights = jax.random.uniform(jax.random.fold_in(jax.random.fold_in(own_key, 6), axis_at), (blocks,), jnp.float32, smallest / len(shards), largest / len(shards))
        gain = gain * jnp.repeat(jnp.exp(heights), dims[axis_at] // blocks).reshape((-1,) + (1,) * (len(dims) - 1 - axis_at))
    return gain


def setup_inputs(seed: int = 0) -> dict:
    seeds = jax.random.split(jax.random.key(seed), 12)
    sky_maps = draw_sky_maps(jax.random.fold_in(seeds[11], 71), 0)
    noise_var = jnp.clip(jnp.exp(math.log(4.0) - 1.3862944 * jax.random.uniform(seeds[1], (LEAVES, P_SIZE), jnp.float32) ** steps_of(seeds[1], (LEAVES, P_SIZE), ((0, 512),), -0.2, 0.2)), 1.0, 4.0)
    position = draw_position(jax.random.fold_in(seeds[11], 71), 0)
    leaf_basis = draw_leaf_basis(jax.random.fold_in(seeds[11], 71), 0)
    leaf_couple = draw_leaf_couple(jax.random.fold_in(seeds[11], 71), 0)
    transfer = draw_transfer(jax.random.fold_in(seeds[11], 71), 0)
    panel_couple = draw_panel_couple(jax.random.fold_in(seeds[11], 71), 0)
    near_list = draw_near_list(jax.random.fold_in(seeds[11], 71), 0)
    far_list = draw_far_list(jax.random.fold_in(seeds[11], 71), 0)
    panel_list = draw_panel_list(jax.random.fold_in(seeds[11], 71), 0)
    leaf_panel = plant(jax.random.randint(seeds[10], (LEAVES,), 0, PANEL_DEV), jax.random.fold_in(seeds[10], 1), 0, PANEL_DEV - 1).astype(jnp.int32)
    return {"sky_maps": sky_maps, "noise_var": noise_var, "position": position, "leaf_basis": leaf_basis, "leaf_couple": leaf_couple, "transfer": transfer, "panel_couple": panel_couple, "near_list": near_list, "far_list": far_list, "panel_list": panel_list, "leaf_panel": leaf_panel}


HIGHEST_PRECISION = lax.Precision.HIGHEST
ROOT_THREE = math.sqrt(3.0)
AMPLITUDE = 0.02

def matern_block(rows_pos, cols_pos, length_scale):
    squared = jnp.zeros((cols_pos.shape[1], rows_pos.shape[1], cols_pos.shape[2]), jnp.float32)
    for component in range(3):
        offset = rows_pos[component][None, :, None] - cols_pos[component][:, None, :]
        squared = squared + offset * offset
    scaled = ROOT_THREE * jnp.sqrt(squared) / length_scale
    return AMPLITUDE * (1.0 + scaled) * jnp.exp(-scaled)

def near_field(values, position, near_list, length_scale):
    map_count = values.shape[0]
    slot_valid = near_list >= 0
    safe_ids = jnp.where(slot_valid, near_list, near_list[:, :1]).astype(jnp.int32)
    slot_mask = slot_valid.astype(jnp.float32)
    block_count = LEAVES // LEAF_DEV
    rows_all = jnp.transpose(position, (1, 0, 2)).reshape(block_count, LEAF_DEV, 3, P_SIZE)
    cols_all = jnp.transpose(position[:, safe_ids], (1, 0, 2, 3)).reshape(block_count, LEAF_DEV, 3, NEAR, P_SIZE)
    vals_all = jnp.transpose(values[:, safe_ids], (1, 0, 2, 3)).reshape(block_count, LEAF_DEV, map_count, NEAR, P_SIZE)
    mask_all = slot_mask.reshape(block_count, LEAF_DEV, NEAR)

    def per_leaf(rows_pos, cols_pos, mask_row, vals_row):
        kernel_block = matern_block(rows_pos, cols_pos, length_scale) * mask_row[:, None, None]
        return jnp.einsum('spq,msq->mp', kernel_block, vals_row, precision=HIGHEST_PRECISION)

    def per_group(leaf_group):
        return jax.vmap(per_leaf)(leaf_group[0], leaf_group[1], leaf_group[2], leaf_group[3])
    result = lax.map(per_group, (rows_all, cols_all, mask_all, vals_all))
    return jnp.transpose(result.reshape(LEAVES, map_count, P_SIZE), (1, 0, 2))

def apply_covariance(values, noise_var, position, leaf_basis, leaf_couple, transfer, panel_couple, near_list, far_list, panel_list, home_panel, length_scale):
    near_part = near_field(values, position, near_list, length_scale)
    coeffs = jnp.einsum('lpr,mlp->mlr', leaf_basis, values, precision=HIGHEST_PRECISION)
    leaf_far = jnp.einsum('lsab,mlsb->mla', leaf_couple, coeffs[:, far_list], precision=HIGHEST_PRECISION)
    upward = jnp.einsum('lab,mla->mlb', transfer, coeffs, precision=HIGHEST_PRECISION)
    panel_coeffs = jnp.zeros((values.shape[0], PANELS, R), jnp.float32).at[:, home_panel].add(upward)
    panel_far = jnp.einsum('ksab,mksb->mka', panel_couple, panel_coeffs[:, panel_list], precision=HIGHEST_PRECISION)
    leaf_far = leaf_far + jnp.einsum('lab,mlb->mla', transfer, panel_far[:, home_panel], precision=HIGHEST_PRECISION)
    far_part = jnp.einsum('lpr,mlr->mlp', leaf_basis, leaf_far, precision=HIGHEST_PRECISION)
    return noise_var[None] * values + near_part + far_part

def reference(sky_maps, noise_var, position, leaf_basis, leaf_couple, transfer, panel_couple, near_list, far_list, panel_list, leaf_panel):
    length_scale = 2.0 * math.pi / CYCLE
    home_panel = (jnp.arange(LEAVES, dtype=jnp.int32) // LEAF_DEV * PANEL_DEV + leaf_panel).astype(jnp.int32)

    def covariance_apply(values):
        return apply_covariance(values, noise_var, position, leaf_basis, leaf_couple, transfer, panel_couple, near_list, far_list, panel_list, home_panel, length_scale)
    solution = jnp.zeros_like(sky_maps)
    residual = sky_maps
    direction = sky_maps
    norm_now = lax.optimization_barrier(jnp.sum(residual * residual, axis=(1, 2)))
    for iteration in range(ITERS):
        applied = covariance_apply(direction)
        step_size = norm_now / lax.optimization_barrier(jnp.sum(direction * applied, axis=(1, 2)))
        solution = solution + step_size[:, None, None] * direction
        residual = residual - step_size[:, None, None] * applied
        if iteration + 1 < ITERS:
            norm_next = lax.optimization_barrier(jnp.sum(residual * residual, axis=(1, 2)))
            direction = residual + (norm_next / norm_now)[:, None, None] * direction
            norm_now = norm_next
    return (solution, residual)
```

```python
import math

import jax
import jax.numpy as jnp
from jax import lax
from jax.sharding import PartitionSpec as P

REACH = 6
ITERS = 2


HIGHEST_PRECISION = lax.Precision.HIGHEST
ROOT_THREE = math.sqrt(3.0)
AMPLITUDE = 0.02


def extended(cells, sides, width):
    for axis, dim in sides:
        count = lax.axis_size(axis)
        head = lax.slice_in_dim(cells, 0, width, axis=dim)
        tail = lax.slice_in_dim(cells, cells.shape[dim] - width, cells.shape[dim], axis=dim)
        cells = jnp.concatenate(
            [
                lax.ppermute(tail, axis, [(i, (i + 1) % count) for i in range(count)]),
                cells,
                lax.ppermute(head, axis, [((i + 1) % count, i) for i in range(count)]),
            ],
            axis=dim,
        )
    return cells


def all_sum(vector, axes):
    for axis in axes:
        count = lax.axis_size(axis)
        if count & (count - 1):
            vector = lax.psum(vector, axis)
            continue
        stride = 1
        while stride < count:
            vector = vector + lax.ppermute(
                vector, axis, [(i, i ^ stride) for i in range(count)]
            )
            stride *= 2
    return vector


def matern_block(rows_pos, cols_pos, length_scale):
    squared = jnp.zeros((cols_pos.shape[1], rows_pos.shape[1], cols_pos.shape[2]), jnp.float32)
    for component in range(3):
        offset = rows_pos[component][None, :, None] - cols_pos[component][:, None, :]
        squared = squared + offset * offset
    scaled = ROOT_THREE * jnp.sqrt(squared) / length_scale
    return AMPLITUDE * (1.0 + scaled) * jnp.exp(-scaled)


def on_device(
    sky_maps,
    noise_var,
    position,
    leaf_basis,
    leaf_couple,
    transfer,
    panel_couple,
    near_list,
    far_list,
    panel_list,
    leaf_panel,
):
    lon_index = lax.axis_index("lon")
    lon_count = lax.axis_size("lon")
    local_leaves = sky_maps.shape[1]
    pixel_count = sky_maps.shape[2]
    cycle_size = local_leaves * lon_count
    panel_count = panel_couple.shape[0]
    length_scale = 2.0 * math.pi / cycle_size
    first_leaf = lon_index * local_leaves
    near_depth = 2

    def rim_index(leaf_ids, depth):
        return (leaf_ids % cycle_size - first_leaf + depth) % cycle_size

    near_valid = near_list >= 0
    near_rows = rim_index(jnp.where(near_valid, near_list, near_list[:, :1]), near_depth)
    far_rows = rim_index(far_list, REACH)
    rim_pos = extended(position, (("lon", 1),), near_depth)

    def leaf_blocks(inputs):
        rows_pos, rows_index, slot_mask = inputs
        cols_pos = rim_pos[:, rows_index]
        return matern_block(rows_pos, cols_pos, length_scale) * slot_mask[:, None, None]

    near_blocks = jax.vmap(lambda *leaf: leaf_blocks(leaf))(
        jnp.transpose(position, (1, 0, 2)), near_rows, near_valid.astype(jnp.float32)
    )
    band_slot = panel_list // (lon_count * panel_count)
    gathered_rows = band_slot * panel_count + panel_list % panel_count
    membership = (leaf_panel[:, None] == jnp.arange(panel_count, dtype=jnp.int32)[None, :]).astype(
        jnp.float32
    )

    def square_total(vector):
        return all_sum(jnp.sum(vector * vector, axis=(1, 2)), ("lon", "band"))

    def covariance_apply(direction):
        coeffs = jnp.einsum("lpr,mlp->mlr", leaf_basis, direction, precision=HIGHEST_PRECISION)
        joined = jnp.concatenate([direction, coeffs], axis=2)
        rim_joined = extended(joined, (("lon", 1),), REACH)
        rim_values = rim_joined[
            :, REACH - near_depth : REACH + local_leaves + near_depth, :pixel_count
        ]
        rim_coeffs = rim_joined[:, :, pixel_count:]
        near_part = jnp.einsum(
            "lspq,mlsq->mlp", near_blocks, rim_values[:, near_rows], precision=HIGHEST_PRECISION
        )
        leaf_far = jnp.einsum(
            "lsab,mlsb->mla", leaf_couple, rim_coeffs[:, far_rows], precision=HIGHEST_PRECISION
        )
        upward = jnp.einsum("lab,mla->mlb", transfer, coeffs, precision=HIGHEST_PRECISION)
        panel_coeffs = jnp.einsum("lk,mlb->mkb", membership, upward, precision=HIGHEST_PRECISION)
        band_coeffs = lax.all_gather(panel_coeffs, "band", axis=1, tiled=True)
        panel_far = jnp.einsum(
            "ksab,mksb->mka",
            panel_couple,
            band_coeffs[:, gathered_rows],
            precision=HIGHEST_PRECISION,
        )
        downward = jnp.einsum("lk,mkb->mlb", membership, panel_far, precision=HIGHEST_PRECISION)
        leaf_far = leaf_far + jnp.einsum(
            "lab,mlb->mla", transfer, downward, precision=HIGHEST_PRECISION
        )
        far_part = jnp.einsum("lpr,mlr->mlp", leaf_basis, leaf_far, precision=HIGHEST_PRECISION)
        return noise_var[None] * direction + near_part + far_part

    solution = jnp.zeros_like(sky_maps)
    residual = sky_maps
    direction = sky_maps
    norm_now = square_total(residual)
    applied = covariance_apply(direction)
    for iteration in range(ITERS):
        curvature_sum = all_sum(jnp.sum(direction * applied, axis=(1, 2)), ("lon", "band"))
        step_size = norm_now / curvature_sum
        solution = solution + step_size[:, None, None] * direction
        residual = residual - step_size[:, None, None] * applied
        if iteration + 1 < ITERS:
            norm_next = square_total(residual)
            applied_residual = covariance_apply(residual)
            ratio = (norm_next / norm_now)[:, None, None]
            direction = residual + ratio * direction
            applied = applied_residual + ratio * applied
            norm_now = norm_next
    return (solution, residual)


def solution(mesh):
    placed = (
        P(None, ("band", "lon"), None),
        P(("band", "lon"), None),
        P(None, ("band", "lon"), None),
        P(("band", "lon"), None, None),
        P(("band", "lon"), None, None, None),
        P(("band", "lon"), None, None),
        P(("band", "lon"), None, None, None),
        P(("band", "lon"), None),
        P(("band", "lon"), None),
        P(("band", "lon"), None),
        P(("band", "lon")),
    )
    return jax.shard_map(
        on_device,
        mesh=mesh,
        in_specs=placed,
        out_specs=(P(None, ("band", "lon"), None), P(None, ("band", "lon"), None)),
        check_vma=False,
    )
```

```python
import math

import jax
import jax.numpy as jnp
from jax import lax
from jax.sharding import PartitionSpec as P

REACH = 6
ITERS = 2


HIGHEST_PRECISION = lax.Precision.HIGHEST
ROOT_THREE = math.sqrt(3.0)
AMPLITUDE = 0.02


def extended(cells, sides, width):
    for axis, dim in sides:
        count = lax.axis_size(axis)
        head = lax.slice_in_dim(cells, 0, width, axis=dim)
        tail = lax.slice_in_dim(cells, cells.shape[dim] - width, cells.shape[dim], axis=dim)
        cells = jnp.concatenate(
            [
                lax.ppermute(tail, axis, [(i, (i + 1) % count) for i in range(count)]),
                cells,
                lax.ppermute(head, axis, [((i + 1) % count, i) for i in range(count)]),
            ],
            axis=dim,
        )
    return cells


def all_sum(vector, axes):
    for axis in axes:
        count = lax.axis_size(axis)
        if count & (count - 1):
            vector = lax.psum(vector, axis)
            continue
        stride = 1
        while stride < count:
            vector = vector + lax.ppermute(
                vector, axis, [(i, i ^ stride) for i in range(count)]
            )
            stride *= 2
    return vector


def matern_block(rows_pos, cols_pos, length_scale):
    squared = jnp.zeros((cols_pos.shape[1], rows_pos.shape[1], cols_pos.shape[2]), jnp.float32)
    for component in range(3):
        offset = rows_pos[component][None, :, None] - cols_pos[component][:, None, :]
        squared = squared + offset * offset
    scaled = ROOT_THREE * jnp.sqrt(squared) / length_scale
    return AMPLITUDE * (1.0 + scaled) * jnp.exp(-scaled)


def on_device(
    sky_maps,
    noise_var,
    position,
    leaf_basis,
    leaf_couple,
    transfer,
    panel_couple,
    near_list,
    far_list,
    panel_list,
    leaf_panel,
):
    lon_index = lax.axis_index("lon")
    lon_count = lax.axis_size("lon")
    local_leaves = sky_maps.shape[1]
    pixel_count = sky_maps.shape[2]
    cycle_size = local_leaves * lon_count
    panel_count = panel_couple.shape[0]
    length_scale = 2.0 * math.pi / cycle_size
    first_leaf = lon_index * local_leaves
    near_depth = 2

    def rim_index(leaf_ids, depth):
        return (leaf_ids % cycle_size - first_leaf + depth) % cycle_size

    near_valid = near_list >= 0
    near_rows = rim_index(jnp.where(near_valid, near_list, near_list[:, :1]), near_depth)
    far_rows = rim_index(far_list, REACH)
    rim_pos = extended(position, (("lon", 1),), near_depth)

    def leaf_blocks(inputs):
        rows_pos, rows_index, slot_mask = inputs
        cols_pos = rim_pos[:, rows_index]
        return matern_block(rows_pos, cols_pos, length_scale) * slot_mask[:, None, None]

    near_blocks = jax.vmap(lambda *leaf: leaf_blocks(leaf))(
        jnp.transpose(position, (1, 0, 2)), near_rows, near_valid.astype(jnp.float32)
    )
    band_slot = panel_list // (lon_count * panel_count)
    gathered_rows = band_slot * panel_count + panel_list % panel_count
    membership = (leaf_panel[:, None] == jnp.arange(panel_count, dtype=jnp.int32)[None, :]).astype(
        jnp.float32
    )

    def covariance_apply(direction):
        coeffs = jnp.einsum("lpr,mlp->mlr", leaf_basis, direction, precision=HIGHEST_PRECISION)
        joined = jnp.concatenate([direction, coeffs], axis=2)
        rim_joined = extended(joined, (("lon", 1),), REACH)
        rim_values = rim_joined[
            :, REACH - near_depth : REACH + local_leaves + near_depth, :pixel_count
        ]
        rim_coeffs = rim_joined[:, :, pixel_count:]
        near_part = jnp.einsum(
            "lspq,mlsq->mlp", near_blocks, rim_values[:, near_rows], precision=HIGHEST_PRECISION
        )
        leaf_far = jnp.einsum(
            "lsab,mlsb->mla", leaf_couple, rim_coeffs[:, far_rows], precision=HIGHEST_PRECISION
        )
        upward = jnp.einsum("lab,mla->mlb", transfer, coeffs, precision=HIGHEST_PRECISION)
        panel_coeffs = jnp.einsum("lk,mlb->mkb", membership, upward, precision=HIGHEST_PRECISION)
        band_coeffs = lax.all_gather(panel_coeffs, "band", axis=1, tiled=True)
        panel_far = jnp.einsum(
            "ksab,mksb->mka",
            panel_couple,
            band_coeffs[:, gathered_rows],
            precision=HIGHEST_PRECISION,
        )
        downward = jnp.einsum("lk,mkb->mlb", membership, panel_far, precision=HIGHEST_PRECISION)
        leaf_far = leaf_far + jnp.einsum(
            "lab,mlb->mla", transfer, downward, precision=HIGHEST_PRECISION
        )
        far_part = jnp.einsum("lpr,mlr->mlp", leaf_basis, leaf_far, precision=HIGHEST_PRECISION)
        return noise_var[None] * direction + near_part + far_part

    def total(*products):
        sums = jnp.stack([jnp.sum(product, axis=(1, 2)) for product in products])
        return all_sum(sums, ("lon", "band"))

    assert ITERS == 2
    direction = sky_maps
    applied = covariance_apply(direction)
    applied_twice = covariance_apply(applied)
    norm_now, curvature_sum = total(direction * direction, direction * applied)
    step_size = (norm_now / curvature_sum)[:, None, None]
    solution = step_size * direction
    residual = direction - step_size * applied
    applied_residual = applied - step_size * applied_twice
    norm_next, residual_curv, cross_one, cross_two = total(
        residual * residual,
        residual * applied_residual,
        residual * applied,
        direction * applied_residual,
    )
    ratio = norm_next / norm_now
    next_curv = residual_curv + ratio * (cross_one + cross_two) + ratio * ratio * curvature_sum
    ratio = ratio[:, None, None]
    step_next = (norm_next / next_curv)[:, None, None]
    solution = solution + step_next * (residual + ratio * direction)
    residual = residual - step_next * (applied_residual + ratio * applied)
    return (solution, residual)


def solution(mesh):
    placed = (
        P(None, ("band", "lon"), None),
        P(("band", "lon"), None),
        P(None, ("band", "lon"), None),
        P(("band", "lon"), None, None),
        P(("band", "lon"), None, None, None),
        P(("band", "lon"), None, None),
        P(("band", "lon"), None, None, None),
        P(("band", "lon"), None),
        P(("band", "lon"), None),
        P(("band", "lon"), None),
        P(("band", "lon")),
    )
    return jax.shard_map(
        on_device,
        mesh=mesh,
        in_specs=placed,
        out_specs=(P(None, ("band", "lon"), None), P(None, ("band", "lon"), None)),
        check_vma=False,
    )
```

```python
import math

import jax
import jax.numpy as jnp
from jax import lax
from jax.sharding import PartitionSpec as P

REACH = 6
ITERS = 2


HIGHEST_PRECISION = lax.Precision.HIGHEST
ROOT_THREE = math.sqrt(3.0)
AMPLITUDE = 0.02


def extended(cells, sides, width):
    for axis, dim in sides:
        count = lax.axis_size(axis)
        head = lax.slice_in_dim(cells, 0, width, axis=dim)
        tail = lax.slice_in_dim(cells, cells.shape[dim] - width, cells.shape[dim], axis=dim)
        cells = jnp.concatenate(
            [
                lax.ppermute(tail, axis, [(i, (i + 1) % count) for i in range(count)]),
                cells,
                lax.ppermute(head, axis, [((i + 1) % count, i) for i in range(count)]),
            ],
            axis=dim,
        )
    return cells


def gathered(vector, axis):
    count = lax.axis_size(axis)
    copies = jnp.broadcast_to(vector[None], (count,) + vector.shape)
    return lax.all_to_all(copies, axis, 0, 0, tiled=False)


def all_sum(vector, axes):
    for axis in axes:
        vector = jnp.sum(gathered(vector, axis), axis=0)
    return vector


def matern_block(rows_pos, cols_pos, length_scale):
    squared = jnp.zeros((cols_pos.shape[1], rows_pos.shape[1], cols_pos.shape[2]), jnp.float32)
    for component in range(3):
        offset = rows_pos[component][None, :, None] - cols_pos[component][:, None, :]
        squared = squared + offset * offset
    scaled = ROOT_THREE * jnp.sqrt(squared) / length_scale
    return AMPLITUDE * (1.0 + scaled) * jnp.exp(-scaled)


def on_device(
    sky_maps,
    noise_var,
    position,
    leaf_basis,
    leaf_couple,
    transfer,
    panel_couple,
    near_list,
    far_list,
    panel_list,
    leaf_panel,
):
    lon_index = lax.axis_index("lon")
    lon_count = lax.axis_size("lon")
    local_leaves = sky_maps.shape[1]
    pixel_count = sky_maps.shape[2]
    cycle_size = local_leaves * lon_count
    panel_count = panel_couple.shape[0]
    length_scale = 2.0 * math.pi / cycle_size
    first_leaf = lon_index * local_leaves
    near_depth = 2

    def rim_index(leaf_ids, depth):
        return (leaf_ids % cycle_size - first_leaf + depth) % cycle_size

    near_valid = near_list >= 0
    near_rows = rim_index(jnp.where(near_valid, near_list, near_list[:, :1]), near_depth)
    far_rows = rim_index(far_list, REACH)
    rim_pos = extended(position, (("lon", 1),), near_depth)

    def leaf_blocks(inputs):
        rows_pos, rows_index, slot_mask = inputs
        cols_pos = rim_pos[:, rows_index]
        return matern_block(rows_pos, cols_pos, length_scale) * slot_mask[:, None, None]

    near_blocks = jax.vmap(lambda *leaf: leaf_blocks(leaf))(
        jnp.transpose(position, (1, 0, 2)), near_rows, near_valid.astype(jnp.float32)
    )
    band_slot = panel_list // (lon_count * panel_count)
    gathered_rows = band_slot * panel_count + panel_list % panel_count
    membership = (leaf_panel[:, None] == jnp.arange(panel_count, dtype=jnp.int32)[None, :]).astype(
        jnp.float32
    )

    def covariance_apply(direction):
        coeffs = jnp.einsum("lpr,mlp->mlr", leaf_basis, direction, precision=HIGHEST_PRECISION)
        joined = jnp.concatenate([direction, coeffs], axis=2)
        rim_joined = extended(joined, (("lon", 1),), REACH)
        rim_values = rim_joined[
            :, REACH - near_depth : REACH + local_leaves + near_depth, :pixel_count
        ]
        rim_coeffs = rim_joined[:, :, pixel_count:]
        near_part = jnp.einsum(
            "lspq,mlsq->mlp", near_blocks, rim_values[:, near_rows], precision=HIGHEST_PRECISION
        )
        leaf_far = jnp.einsum(
            "lsab,mlsb->mla", leaf_couple, rim_coeffs[:, far_rows], precision=HIGHEST_PRECISION
        )
        upward = jnp.einsum("lab,mla->mlb", transfer, coeffs, precision=HIGHEST_PRECISION)
        panel_coeffs = jnp.einsum("lk,mlb->mkb", membership, upward, precision=HIGHEST_PRECISION)
        band_coeffs = jnp.swapaxes(gathered(panel_coeffs, "band"), 0, 1).reshape(
            panel_coeffs.shape[0], -1, panel_coeffs.shape[2]
        )
        panel_far = jnp.einsum(
            "ksab,mksb->mka",
            panel_couple,
            band_coeffs[:, gathered_rows],
            precision=HIGHEST_PRECISION,
        )
        downward = jnp.einsum("lk,mkb->mlb", membership, panel_far, precision=HIGHEST_PRECISION)
        leaf_far = leaf_far + jnp.einsum(
            "lab,mlb->mla", transfer, downward, precision=HIGHEST_PRECISION
        )
        far_part = jnp.einsum("lpr,mlr->mlp", leaf_basis, leaf_far, precision=HIGHEST_PRECISION)
        return noise_var[None] * direction + near_part + far_part

    def total(*products):
        sums = jnp.stack([jnp.sum(product, axis=(1, 2)) for product in products])
        return all_sum(sums, ("lon", "band"))

    assert ITERS == 2
    direction = sky_maps
    applied = covariance_apply(direction)
    applied_twice = covariance_apply(applied)
    norm_now, curvature_sum = total(direction * direction, direction * applied)
    step_size = (norm_now / curvature_sum)[:, None, None]
    solution = step_size * direction
    residual = direction - step_size * applied
    applied_residual = applied - step_size * applied_twice
    norm_next, residual_curv, cross_one, cross_two = total(
        residual * residual,
        residual * applied_residual,
        residual * applied,
        direction * applied_residual,
    )
    ratio = norm_next / norm_now
    next_curv = residual_curv + ratio * (cross_one + cross_two) + ratio * ratio * curvature_sum
    ratio = ratio[:, None, None]
    step_next = (norm_next / next_curv)[:, None, None]
    solution = solution + step_next * (residual + ratio * direction)
    residual = residual - step_next * (applied_residual + ratio * applied)
    return (solution, residual)


def solution(mesh):
    placed = (
        P(None, ("band", "lon"), None),
        P(("band", "lon"), None),
        P(None, ("band", "lon"), None),
        P(("band", "lon"), None, None),
        P(("band", "lon"), None, None, None),
        P(("band", "lon"), None, None),
        P(("band", "lon"), None, None, None),
        P(("band", "lon"), None),
        P(("band", "lon"), None),
        P(("band", "lon"), None),
        P(("band", "lon")),
    )
    return jax.shard_map(
        on_device,
        mesh=mesh,
        in_specs=placed,
        out_specs=(P(None, ("band", "lon"), None), P(None, ("band", "lon"), None)),
        check_vma=False,
    )
```

```python
import math

import jax
import jax.numpy as jnp
from jax import lax
from jax.sharding import PartitionSpec as P

REACH = 6
ITERS = 2


HIGHEST_PRECISION = lax.Precision.HIGHEST
ROOT_THREE = math.sqrt(3.0)
AMPLITUDE = 0.02


def extended(cells, sides, width):
    for axis, dim in sides:
        count = lax.axis_size(axis)
        head = lax.slice_in_dim(cells, 0, width, axis=dim)
        tail = lax.slice_in_dim(cells, cells.shape[dim] - width, cells.shape[dim], axis=dim)
        cells = jnp.concatenate(
            [
                lax.ppermute(tail, axis, [(i, (i + 1) % count) for i in range(count)]),
                cells,
                lax.ppermute(head, axis, [((i + 1) % count, i) for i in range(count)]),
            ],
            axis=dim,
        )
    return cells


def gathered(vector, axis):
    count = lax.axis_size(axis)
    copies = jnp.broadcast_to(vector[None], (count,) + vector.shape)
    return lax.all_to_all(copies, axis, 0, 0, tiled=False)


def all_sum(vector, axes):
    for axis in axes:
        vector = jnp.sum(gathered(vector, axis), axis=0)
    return vector


def matern_shape(rows_pos, cols_pos, length_scale):
    squared = None
    for component in range(3):
        offset = rows_pos[component][None, :, None] - cols_pos[component][:, None, :]
        squared = offset * offset if squared is None else squared + offset * offset
    scaled = jnp.sqrt(squared) * (ROOT_THREE / length_scale)
    return (1.0 + scaled) * jnp.exp(-scaled)


def on_device(
    sky_maps,
    noise_var,
    position,
    leaf_basis,
    leaf_couple,
    transfer,
    panel_couple,
    near_list,
    far_list,
    panel_list,
    leaf_panel,
):
    lon_index = lax.axis_index("lon")
    lon_count = lax.axis_size("lon")
    local_leaves = sky_maps.shape[1]
    pixel_count = sky_maps.shape[2]
    cycle_size = local_leaves * lon_count
    panel_count = panel_couple.shape[0]
    length_scale = 2.0 * math.pi / cycle_size
    first_leaf = lon_index * local_leaves
    near_depth = 2

    def rim_index(leaf_ids, depth):
        return (leaf_ids % cycle_size - first_leaf + depth) % cycle_size

    near_valid = near_list >= 0
    near_rows = rim_index(jnp.where(near_valid, near_list, near_list[:, :1]), near_depth)
    far_rows = rim_index(far_list, REACH)
    rim_pos = extended(position, (("lon", 1),), near_depth)

    def leaf_blocks(rows_pos, rows_index):
        return matern_shape(rows_pos, rim_pos[:, rows_index], length_scale)

    near_blocks = jax.vmap(leaf_blocks)(jnp.transpose(position, (1, 0, 2)), near_rows)
    slot_scale = AMPLITUDE * near_valid.astype(jnp.float32)
    band_slot = panel_list // (lon_count * panel_count)
    gathered_rows = band_slot * panel_count + panel_list % panel_count
    membership = (leaf_panel[:, None] == jnp.arange(panel_count, dtype=jnp.int32)[None, :]).astype(
        jnp.float32
    )

    def covariance_apply(direction):
        coeffs = jnp.einsum("lpr,mlp->mlr", leaf_basis, direction, precision=HIGHEST_PRECISION)
        joined = jnp.concatenate([direction, coeffs], axis=2)
        rim_joined = extended(joined, (("lon", 1),), REACH)
        rim_values = rim_joined[
            :, REACH - near_depth : REACH + local_leaves + near_depth, :pixel_count
        ]
        rim_coeffs = rim_joined[:, :, pixel_count:]
        near_values = rim_values[:, near_rows] * slot_scale[None, :, :, None]
        near_part = jnp.einsum(
            "lspq,mlsq->mlp", near_blocks, near_values, precision=lax.Precision.HIGH
        )
        leaf_far = jnp.einsum(
            "lsab,mlsb->mla", leaf_couple, rim_coeffs[:, far_rows], precision=HIGHEST_PRECISION
        )
        upward = jnp.einsum("lab,mla->mlb", transfer, coeffs, precision=HIGHEST_PRECISION)
        panel_coeffs = jnp.einsum("lk,mlb->mkb", membership, upward, precision=HIGHEST_PRECISION)
        band_coeffs = jnp.swapaxes(gathered(panel_coeffs, "band"), 0, 1).reshape(
            panel_coeffs.shape[0], -1, panel_coeffs.shape[2]
        )
        panel_far = jnp.einsum(
            "ksab,mksb->mka",
            panel_couple,
            band_coeffs[:, gathered_rows],
            precision=HIGHEST_PRECISION,
        )
        downward = jnp.einsum("lk,mkb->mlb", membership, panel_far, precision=HIGHEST_PRECISION)
        leaf_far = leaf_far + jnp.einsum(
            "lab,mlb->mla", transfer, downward, precision=HIGHEST_PRECISION
        )
        far_part = jnp.einsum("lpr,mlr->mlp", leaf_basis, leaf_far, precision=HIGHEST_PRECISION)
        return noise_var[None] * direction + near_part + far_part

    def total(*products):
        sums = jnp.stack([jnp.sum(product, axis=(1, 2)) for product in products])
        return all_sum(sums, ("lon", "band"))

    assert ITERS == 2
    direction = sky_maps
    applied = covariance_apply(direction)
    applied_twice = covariance_apply(applied)
    norm_now, curvature_sum = total(direction * direction, direction * applied)
    step_size = (norm_now / curvature_sum)[:, None, None]
    solution = step_size * direction
    residual = direction - step_size * applied
    applied_residual = applied - step_size * applied_twice
    norm_next, residual_curv, cross_one, cross_two = total(
        residual * residual,
        residual * applied_residual,
        residual * applied,
        direction * applied_residual,
    )
    ratio = norm_next / norm_now
    next_curv = residual_curv + ratio * (cross_one + cross_two) + ratio * ratio * curvature_sum
    ratio = ratio[:, None, None]
    step_next = (norm_next / next_curv)[:, None, None]
    solution = solution + step_next * (residual + ratio * direction)
    residual = residual - step_next * (applied_residual + ratio * applied)
    return (solution, residual)


def solution(mesh):
    placed = (
        P(None, ("band", "lon"), None),
        P(("band", "lon"), None),
        P(None, ("band", "lon"), None),
        P(("band", "lon"), None, None),
        P(("band", "lon"), None, None, None),
        P(("band", "lon"), None, None),
        P(("band", "lon"), None, None, None),
        P(("band", "lon"), None),
        P(("band", "lon"), None),
        P(("band", "lon"), None),
        P(("band", "lon")),
    )
    return jax.shard_map(
        on_device,
        mesh=mesh,
        in_specs=placed,
        out_specs=(P(None, ("band", "lon"), None), P(None, ("band", "lon"), None)),
        check_vma=False,
    )
```

```python
import math

import jax
import jax.numpy as jnp
from jax import lax
from jax.sharding import PartitionSpec as P

REACH = 6
ITERS = 2


HIGHEST_PRECISION = lax.Precision.HIGHEST
ROOT_THREE = math.sqrt(3.0)
AMPLITUDE = 0.02


def extended(cells, sides, width):
    for axis, dim in sides:
        count = lax.axis_size(axis)
        head = lax.slice_in_dim(cells, 0, width, axis=dim)
        tail = lax.slice_in_dim(cells, cells.shape[dim] - width, cells.shape[dim], axis=dim)
        cells = jnp.concatenate(
            [
                lax.ppermute(tail, axis, [(i, (i + 1) % count) for i in range(count)]),
                cells,
                lax.ppermute(head, axis, [((i + 1) % count, i) for i in range(count)]),
            ],
            axis=dim,
        )
    return cells


def gathered(vector, axis):
    count = lax.axis_size(axis)
    copies = jnp.broadcast_to(vector[None], (count,) + vector.shape)
    return lax.all_to_all(copies, axis, 0, 0, tiled=False)


def all_sum(vector, axes):
    for axis in axes:
        vector = jnp.sum(gathered(vector, axis), axis=0)
    return vector


def matern_shape(rows_pos, cols_pos, length_scale):
    squared = None
    for component in range(3):
        offset = rows_pos[component][:, :, None] - cols_pos[component][:, None, :]
        squared = offset * offset if squared is None else squared + offset * offset
    scaled = jnp.sqrt(squared) * (ROOT_THREE / length_scale)
    return (1.0 + scaled) * jnp.exp(-scaled)


def on_device(
    sky_maps,
    noise_var,
    position,
    leaf_basis,
    leaf_couple,
    transfer,
    panel_couple,
    near_list,
    far_list,
    panel_list,
    leaf_panel,
):
    lon_index = lax.axis_index("lon")
    lon_count = lax.axis_size("lon")
    local_leaves = sky_maps.shape[1]
    pixel_count = sky_maps.shape[2]
    cycle_size = local_leaves * lon_count
    panel_count = panel_couple.shape[0]
    length_scale = 2.0 * math.pi / cycle_size
    first_leaf = lon_index * local_leaves
    near_depth = 2

    def rim_index(leaf_ids, depth):
        return (leaf_ids % cycle_size - first_leaf + depth) % cycle_size

    near_valid = near_list >= 0
    near_rows = rim_index(jnp.where(near_valid, near_list, near_list[:, :1]), near_depth)
    far_rows = rim_index(far_list, REACH)
    rim_pos = extended(position, (("lon", 1),), near_depth)

    same_blocks = matern_shape(
        rim_pos[:, near_depth : near_depth + local_leaves],
        rim_pos[:, near_depth : near_depth + local_leaves],
        length_scale,
    )
    step_blocks = [
        matern_shape(
            rim_pos[:, near_depth - step : near_depth + local_leaves],
            rim_pos[:, near_depth : near_depth + local_leaves + step],
            length_scale,
        )
        for step in range(1, near_depth + 1)
    ]
    step_range = jnp.arange(-near_depth, near_depth + 1, dtype=jnp.int32)
    targets = jnp.arange(local_leaves, dtype=jnp.int32)[:, None] + near_depth + step_range[None, :]
    matches = (near_rows[:, :, None] == targets[:, None, :]) & near_valid[:, :, None]
    offset_scale = AMPLITUDE * jnp.sum(matches.astype(jnp.float32), axis=1)
    band_slot = panel_list // (lon_count * panel_count)
    gathered_rows = band_slot * panel_count + panel_list % panel_count
    membership = (leaf_panel[:, None] == jnp.arange(panel_count, dtype=jnp.int32)[None, :]).astype(
        jnp.float32
    )

    def covariance_apply(direction):
        coeffs = jnp.einsum("lpr,mlp->mlr", leaf_basis, direction, precision=HIGHEST_PRECISION)
        joined = jnp.concatenate([direction, coeffs], axis=2)
        rim_joined = extended(joined, (("lon", 1),), REACH)
        rim_values = rim_joined[
            :, REACH - near_depth : REACH + local_leaves + near_depth, :pixel_count
        ]
        rim_coeffs = rim_joined[:, :, pixel_count:]

        def offset_values(step):
            start = near_depth + step
            values = rim_values[:, start : start + local_leaves]
            return values * offset_scale[None, :, step + near_depth, None]

        near_part = jnp.einsum(
            "ipq,miq->mip", same_blocks, offset_values(0), precision=lax.Precision.HIGH
        )
        for step in range(1, near_depth + 1):
            blocks = step_blocks[step - 1]
            ahead = blocks[step : step + local_leaves]
            behind = blocks[:local_leaves]
            near_part = near_part + jnp.einsum(
                "ipq,miq->mip", ahead, offset_values(step), precision=lax.Precision.HIGH
            )
            near_part = near_part + jnp.einsum(
                "iqp,miq->mip", behind, offset_values(-step), precision=lax.Precision.HIGH
            )
        leaf_far = jnp.einsum(
            "lsab,mlsb->mla", leaf_couple, rim_coeffs[:, far_rows], precision=HIGHEST_PRECISION
        )
        upward = jnp.einsum("lab,mla->mlb", transfer, coeffs, precision=HIGHEST_PRECISION)
        panel_coeffs = jnp.einsum("lk,mlb->mkb", membership, upward, precision=HIGHEST_PRECISION)
        band_coeffs = jnp.swapaxes(gathered(panel_coeffs, "band"), 0, 1).reshape(
            panel_coeffs.shape[0], -1, panel_coeffs.shape[2]
        )
        panel_far = jnp.einsum(
            "ksab,mksb->mka",
            panel_couple,
            band_coeffs[:, gathered_rows],
            precision=HIGHEST_PRECISION,
        )
        downward = jnp.einsum("lk,mkb->mlb", membership, panel_far, precision=HIGHEST_PRECISION)
        leaf_far = leaf_far + jnp.einsum(
            "lab,mlb->mla", transfer, downward, precision=HIGHEST_PRECISION
        )
        far_part = jnp.einsum("lpr,mlr->mlp", leaf_basis, leaf_far, precision=HIGHEST_PRECISION)
        return noise_var[None] * direction + near_part + far_part

    def total(*products):
        sums = jnp.stack([jnp.sum(product, axis=(1, 2)) for product in products])
        return all_sum(sums, ("lon", "band"))

    assert ITERS == 2
    direction = sky_maps
    applied = covariance_apply(direction)
    applied_twice = covariance_apply(applied)
    norm_now, curvature_sum = total(direction * direction, direction * applied)
    step_size = (norm_now / curvature_sum)[:, None, None]
    solution = step_size * direction
    residual = direction - step_size * applied
    applied_residual = applied - step_size * applied_twice
    norm_next, residual_curv, cross_one, cross_two = total(
        residual * residual,
        residual * applied_residual,
        residual * applied,
        direction * applied_residual,
    )
    ratio = norm_next / norm_now
    next_curv = residual_curv + ratio * (cross_one + cross_two) + ratio * ratio * curvature_sum
    ratio = ratio[:, None, None]
    step_next = (norm_next / next_curv)[:, None, None]
    solution = solution + step_next * (residual + ratio * direction)
    residual = residual - step_next * (applied_residual + ratio * applied)
    return (solution, residual)


def solution(mesh):
    placed = (
        P(None, ("band", "lon"), None),
        P(("band", "lon"), None),
        P(None, ("band", "lon"), None),
        P(("band", "lon"), None, None),
        P(("band", "lon"), None, None, None),
        P(("band", "lon"), None, None),
        P(("band", "lon"), None, None, None),
        P(("band", "lon"), None),
        P(("band", "lon"), None),
        P(("band", "lon"), None),
        P(("band", "lon")),
    )
    return jax.shard_map(
        on_device,
        mesh=mesh,
        in_specs=placed,
        out_specs=(P(None, ("band", "lon"), None), P(None, ("band", "lon"), None)),
        check_vma=False,
    )
```

```python
import math

import jax
import jax.numpy as jnp
from jax import lax
from jax.sharding import PartitionSpec as P

REACH = 6
ITERS = 2


HIGHEST_PRECISION = lax.Precision.HIGHEST
ROOT_THREE = math.sqrt(3.0)
AMPLITUDE = 0.02


def extended(cells, sides, width):
    for axis, dim in sides:
        count = lax.axis_size(axis)
        head = lax.slice_in_dim(cells, 0, width, axis=dim)
        tail = lax.slice_in_dim(cells, cells.shape[dim] - width, cells.shape[dim], axis=dim)
        cells = jnp.concatenate(
            [
                lax.ppermute(tail, axis, [(i, (i + 1) % count) for i in range(count)]),
                cells,
                lax.ppermute(head, axis, [((i + 1) % count, i) for i in range(count)]),
            ],
            axis=dim,
        )
    return cells


def gathered(vector, axis):
    count = lax.axis_size(axis)
    copies = jnp.broadcast_to(vector[None], (count,) + vector.shape)
    return lax.all_to_all(copies, axis, 0, 0, tiled=False)


def all_sum(vector, axes):
    for axis in axes:
        vector = jnp.sum(gathered(vector, axis), axis=0)
    return vector


def matern_shape(rows_pos, cols_pos, length_scale):
    squared = None
    for component in range(3):
        offset = rows_pos[component][:, :, None] - cols_pos[component][:, None, :]
        squared = offset * offset if squared is None else squared + offset * offset
    scaled = jnp.sqrt(squared) * (ROOT_THREE / length_scale)
    return (1.0 + scaled) * jnp.exp(-scaled)


def on_device(
    sky_maps,
    noise_var,
    position,
    leaf_basis,
    leaf_couple,
    transfer,
    panel_couple,
    near_list,
    far_list,
    panel_list,
    leaf_panel,
):
    lon_index = lax.axis_index("lon")
    lon_count = lax.axis_size("lon")
    local_leaves = sky_maps.shape[1]
    pixel_count = sky_maps.shape[2]
    cycle_size = local_leaves * lon_count
    panel_count = panel_couple.shape[0]
    length_scale = 2.0 * math.pi / cycle_size
    first_leaf = lon_index * local_leaves
    near_depth = 2

    def rim_index(leaf_ids, depth):
        return (leaf_ids % cycle_size - first_leaf + depth) % cycle_size

    near_valid = near_list >= 0
    near_rows = rim_index(jnp.where(near_valid, near_list, near_list[:, :1]), near_depth)
    far_rows = rim_index(far_list, REACH)
    rim_pos = extended(position, (("lon", 1),), near_depth)

    same_blocks = matern_shape(
        rim_pos[:, near_depth : near_depth + local_leaves],
        rim_pos[:, near_depth : near_depth + local_leaves],
        length_scale,
    )
    step_blocks = [
        matern_shape(
            rim_pos[:, near_depth - step : near_depth + local_leaves],
            rim_pos[:, near_depth : near_depth + local_leaves + step],
            length_scale,
        )
        for step in range(1, near_depth + 1)
    ]
    step_range = jnp.arange(-near_depth, near_depth + 1, dtype=jnp.int32)
    targets = jnp.arange(local_leaves, dtype=jnp.int32)[:, None] + near_depth + step_range[None, :]
    matches = (near_rows[:, :, None] == targets[:, None, :]) & near_valid[:, :, None]
    offset_scale = AMPLITUDE * jnp.sum(matches.astype(jnp.float32), axis=1)
    band_slot = panel_list // (lon_count * panel_count)
    gathered_rows = band_slot * panel_count + panel_list % panel_count
    membership = (leaf_panel[:, None] == jnp.arange(panel_count, dtype=jnp.int32)[None, :]).astype(
        jnp.float32
    )

    def covariance_local(direction):
        coeffs = jnp.einsum("lpr,mlp->mlr", leaf_basis, direction, precision=HIGHEST_PRECISION)
        joined = jnp.concatenate([direction, coeffs], axis=2)
        rim_joined = extended(joined, (("lon", 1),), REACH)
        rim_values = rim_joined[
            :, REACH - near_depth : REACH + local_leaves + near_depth, :pixel_count
        ]
        rim_coeffs = rim_joined[:, :, pixel_count:]

        def offset_values(step):
            start = near_depth + step
            values = rim_values[:, start : start + local_leaves]
            return values * offset_scale[None, :, step + near_depth, None]

        near_part = jnp.einsum(
            "ipq,miq->mip", same_blocks, offset_values(0), precision=lax.Precision.HIGH
        )
        for step in range(1, near_depth + 1):
            blocks = step_blocks[step - 1]
            ahead = blocks[step : step + local_leaves]
            behind = blocks[:local_leaves]
            near_part = near_part + jnp.einsum(
                "ipq,miq->mip", ahead, offset_values(step), precision=lax.Precision.HIGH
            )
            near_part = near_part + jnp.einsum(
                "iqp,miq->mip", behind, offset_values(-step), precision=lax.Precision.HIGH
            )
        leaf_far = jnp.einsum(
            "lsab,mlsb->mla", leaf_couple, rim_coeffs[:, far_rows], precision=HIGHEST_PRECISION
        )
        upward = jnp.einsum("lab,mla->mlb", transfer, coeffs, precision=HIGHEST_PRECISION)
        panel_coeffs = jnp.einsum("lk,mlb->mkb", membership, upward, precision=HIGHEST_PRECISION)
        return direction, near_part, leaf_far, panel_coeffs

    def band_layout(band_panels, panel_coeffs):
        stacked = band_panels.reshape((band_panels.shape[0],) + panel_coeffs.shape)
        return jnp.swapaxes(stacked, 0, 1).reshape(
            panel_coeffs.shape[0], -1, panel_coeffs.shape[2]
        )

    def covariance_finish(local, band_coeffs):
        direction, near_part, leaf_far, panel_coeffs = local
        panel_far = jnp.einsum(
            "ksab,mksb->mka",
            panel_couple,
            band_coeffs[:, gathered_rows],
            precision=HIGHEST_PRECISION,
        )
        downward = jnp.einsum("lk,mkb->mlb", membership, panel_far, precision=HIGHEST_PRECISION)
        leaf_far = leaf_far + jnp.einsum(
            "lab,mlb->mla", transfer, downward, precision=HIGHEST_PRECISION
        )
        far_part = jnp.einsum("lpr,mlr->mlp", leaf_basis, leaf_far, precision=HIGHEST_PRECISION)
        return noise_var[None] * direction + near_part + far_part

    def covariance_apply(direction):
        local = covariance_local(direction)
        panel_coeffs = local[3]
        band_panels = gathered(panel_coeffs.reshape(-1), "band")
        return covariance_finish(local, band_layout(band_panels, panel_coeffs))

    def total(*products):
        sums = jnp.stack([jnp.sum(product, axis=(1, 2)) for product in products])
        return all_sum(sums, ("lon", "band"))

    assert ITERS == 2
    direction = sky_maps
    applied = covariance_apply(direction)
    applied_local = covariance_local(applied)
    first_sums = jnp.stack(
        [jnp.sum(product, axis=(1, 2)) for product in (direction * direction, direction * applied)]
    )
    first_sums = all_sum(first_sums, ("lon",))
    panel_coeffs = applied_local[3]
    payload = jnp.concatenate([panel_coeffs.reshape(-1), first_sums.reshape(-1)])
    band_payload = gathered(payload, "band")
    panel_size = panel_coeffs.size
    norm_now, curvature_sum = jnp.sum(band_payload[:, panel_size:], axis=0).reshape(
        first_sums.shape
    )
    applied_twice = covariance_finish(
        applied_local, band_layout(band_payload[:, :panel_size], panel_coeffs)
    )
    step_size = (norm_now / curvature_sum)[:, None, None]
    solution = step_size * direction
    residual = direction - step_size * applied
    applied_residual = applied - step_size * applied_twice
    norm_next, residual_curv, cross_one, cross_two = total(
        residual * residual,
        residual * applied_residual,
        residual * applied,
        direction * applied_residual,
    )
    ratio = norm_next / norm_now
    next_curv = residual_curv + ratio * (cross_one + cross_two) + ratio * ratio * curvature_sum
    ratio = ratio[:, None, None]
    step_next = (norm_next / next_curv)[:, None, None]
    solution = solution + step_next * (residual + ratio * direction)
    residual = residual - step_next * (applied_residual + ratio * applied)
    return (solution, residual)


def solution(mesh):
    placed = (
        P(None, ("band", "lon"), None),
        P(("band", "lon"), None),
        P(None, ("band", "lon"), None),
        P(("band", "lon"), None, None),
        P(("band", "lon"), None, None, None),
        P(("band", "lon"), None, None),
        P(("band", "lon"), None, None, None),
        P(("band", "lon"), None),
        P(("band", "lon"), None),
        P(("band", "lon"), None),
        P(("band", "lon")),
    )
    return jax.shard_map(
        on_device,
        mesh=mesh,
        in_specs=placed,
        out_specs=(P(None, ("band", "lon"), None), P(None, ("band", "lon"), None)),
        check_vma=False,
    )
```

```python
import math

import jax
import jax.numpy as jnp
from jax import lax
from jax.sharding import PartitionSpec as P

REACH = 6
ITERS = 2


HIGHEST_PRECISION = lax.Precision.HIGHEST
ROOT_THREE = math.sqrt(3.0)
AMPLITUDE = 0.02


def extended_together(items, axis):
    count = lax.axis_size(axis)
    heads = [lax.slice_in_dim(cells, 0, width, axis=dim) for cells, dim, width in items]
    tails = [
        lax.slice_in_dim(cells, cells.shape[dim] - width, cells.shape[dim], axis=dim)
        for cells, dim, width in items
    ]

    def moved(parts, pairs):
        flat = lax.ppermute(jnp.concatenate([part.reshape(-1) for part in parts]), axis, pairs)
        pieces, start = [], 0
        for part in parts:
            pieces.append(flat[start : start + part.size].reshape(part.shape))
            start += part.size
        return pieces

    from_before = moved(tails, [(i, (i + 1) % count) for i in range(count)])
    from_after = moved(heads, [((i + 1) % count, i) for i in range(count)])
    return [
        jnp.concatenate([before, cells, after], axis=dim)
        for (cells, dim, _), before, after in zip(items, from_before, from_after)
    ]


def gathered(vector, axis):
    count = lax.axis_size(axis)
    copies = jnp.broadcast_to(vector[None], (count,) + vector.shape)
    return lax.all_to_all(copies, axis, 0, 0, tiled=False)


def all_sum(vector, axes):
    for axis in axes:
        vector = jnp.sum(gathered(vector, axis), axis=0)
    return vector


def matern_shape(rows_pos, cols_pos, length_scale):
    squared = None
    for component in range(3):
        offset = rows_pos[component][:, :, None] - cols_pos[component][:, None, :]
        squared = offset * offset if squared is None else squared + offset * offset
    scaled = jnp.sqrt(squared) * (ROOT_THREE / length_scale)
    return (1.0 + scaled) * jnp.exp(-scaled)


def on_device(
    sky_maps,
    noise_var,
    position,
    leaf_basis,
    leaf_couple,
    transfer,
    panel_couple,
    near_list,
    far_list,
    panel_list,
    leaf_panel,
):
    lon_index = lax.axis_index("lon")
    lon_count = lax.axis_size("lon")
    local_leaves = sky_maps.shape[1]
    pixel_count = sky_maps.shape[2]
    cycle_size = local_leaves * lon_count
    panel_count = panel_couple.shape[0]
    length_scale = 2.0 * math.pi / cycle_size
    first_leaf = lon_index * local_leaves
    near_depth = 2

    def rim_index(leaf_ids, depth):
        return (leaf_ids % cycle_size - first_leaf + depth) % cycle_size

    near_valid = near_list >= 0
    near_rows = rim_index(jnp.where(near_valid, near_list, near_list[:, :1]), near_depth)
    far_rows = rim_index(far_list, REACH)

    def near_blocks(rim_pos):
        same_blocks = matern_shape(
            rim_pos[:, near_depth : near_depth + local_leaves],
            rim_pos[:, near_depth : near_depth + local_leaves],
            length_scale,
        )
        step_blocks = [
            matern_shape(
                rim_pos[:, near_depth - step : near_depth + local_leaves],
                rim_pos[:, near_depth : near_depth + local_leaves + step],
                length_scale,
            )
            for step in range(1, near_depth + 1)
        ]
        return same_blocks, step_blocks

    step_range = jnp.arange(-near_depth, near_depth + 1, dtype=jnp.int32)
    targets = jnp.arange(local_leaves, dtype=jnp.int32)[:, None] + near_depth + step_range[None, :]
    matches = (near_rows[:, :, None] == targets[:, None, :]) & near_valid[:, :, None]
    offset_scale = AMPLITUDE * jnp.sum(matches.astype(jnp.float32), axis=1)
    band_slot = panel_list // (lon_count * panel_count)
    gathered_rows = band_slot * panel_count + panel_list % panel_count
    membership = (leaf_panel[:, None] == jnp.arange(panel_count, dtype=jnp.int32)[None, :]).astype(
        jnp.float32
    )

    def covariance_local(direction, blocks=None):
        coeffs = jnp.einsum("lpr,mlp->mlr", leaf_basis, direction, precision=HIGHEST_PRECISION)
        joined = jnp.concatenate([direction, coeffs], axis=2)
        items = [(joined, 1, REACH)]
        if blocks is None:
            items.append((position, 1, near_depth))
        rims = extended_together(items, "lon")
        rim_joined = rims[0]
        if blocks is None:
            blocks = near_blocks(rims[1])
        same_blocks, step_blocks = blocks
        rim_values = rim_joined[
            :, REACH - near_depth : REACH + local_leaves + near_depth, :pixel_count
        ]
        rim_coeffs = rim_joined[:, :, pixel_count:]

        def offset_values(step):
            start = near_depth + step
            values = rim_values[:, start : start + local_leaves]
            return values * offset_scale[None, :, step + near_depth, None]

        near_part = jnp.einsum(
            "ipq,miq->mip", same_blocks, offset_values(0), precision=lax.Precision.HIGH
        )
        for step in range(1, near_depth + 1):
            step_block = step_blocks[step - 1]
            ahead = step_block[step : step + local_leaves]
            behind = step_block[:local_leaves]
            near_part = near_part + jnp.einsum(
                "ipq,miq->mip", ahead, offset_values(step), precision=lax.Precision.HIGH
            )
            near_part = near_part + jnp.einsum(
                "iqp,miq->mip", behind, offset_values(-step), precision=lax.Precision.HIGH
            )
        leaf_far = jnp.einsum(
            "lsab,mlsb->mla", leaf_couple, rim_coeffs[:, far_rows], precision=HIGHEST_PRECISION
        )
        upward = jnp.einsum("lab,mla->mlb", transfer, coeffs, precision=HIGHEST_PRECISION)
        panel_coeffs = jnp.einsum("lk,mlb->mkb", membership, upward, precision=HIGHEST_PRECISION)
        return (direction, near_part, leaf_far, panel_coeffs), blocks

    def band_layout(band_panels, panel_coeffs):
        stacked = band_panels.reshape((band_panels.shape[0],) + panel_coeffs.shape)
        return jnp.swapaxes(stacked, 0, 1).reshape(
            panel_coeffs.shape[0], -1, panel_coeffs.shape[2]
        )

    def covariance_finish(local, band_coeffs):
        direction, near_part, leaf_far, panel_coeffs = local
        panel_far = jnp.einsum(
            "ksab,mksb->mka",
            panel_couple,
            band_coeffs[:, gathered_rows],
            precision=HIGHEST_PRECISION,
        )
        downward = jnp.einsum("lk,mkb->mlb", membership, panel_far, precision=HIGHEST_PRECISION)
        leaf_far = leaf_far + jnp.einsum(
            "lab,mlb->mla", transfer, downward, precision=HIGHEST_PRECISION
        )
        far_part = jnp.einsum("lpr,mlr->mlp", leaf_basis, leaf_far, precision=HIGHEST_PRECISION)
        return noise_var[None] * direction + near_part + far_part

    def covariance_apply(direction):
        local, blocks = covariance_local(direction)
        panel_coeffs = local[3]
        band_panels = gathered(panel_coeffs.reshape(-1), "band")
        return covariance_finish(local, band_layout(band_panels, panel_coeffs)), blocks

    def total(*products):
        sums = jnp.stack([jnp.sum(product, axis=(1, 2)) for product in products])
        return all_sum(sums, ("lon", "band"))

    assert ITERS == 2
    direction = sky_maps
    applied, blocks = covariance_apply(direction)
    applied_local, _ = covariance_local(applied, blocks)
    first_sums = jnp.stack(
        [jnp.sum(product, axis=(1, 2)) for product in (direction * direction, direction * applied)]
    )
    first_sums = all_sum(first_sums, ("lon",))
    panel_coeffs = applied_local[3]
    payload = jnp.concatenate([panel_coeffs.reshape(-1), first_sums.reshape(-1)])
    band_payload = gathered(payload, "band")
    panel_size = panel_coeffs.size
    norm_now, curvature_sum = jnp.sum(band_payload[:, panel_size:], axis=0).reshape(
        first_sums.shape
    )
    applied_twice = covariance_finish(
        applied_local, band_layout(band_payload[:, :panel_size], panel_coeffs)
    )
    step_size = (norm_now / curvature_sum)[:, None, None]
    solution = step_size * direction
    residual = direction - step_size * applied
    applied_residual = applied - step_size * applied_twice
    norm_next, residual_curv, cross_one, cross_two = total(
        residual * residual,
        residual * applied_residual,
        residual * applied,
        direction * applied_residual,
    )
    ratio = norm_next / norm_now
    next_curv = residual_curv + ratio * (cross_one + cross_two) + ratio * ratio * curvature_sum
    ratio = ratio[:, None, None]
    step_next = (norm_next / next_curv)[:, None, None]
    solution = solution + step_next * (residual + ratio * direction)
    residual = residual - step_next * (applied_residual + ratio * applied)
    return (solution, residual)


def solution(mesh):
    placed = (
        P(None, ("band", "lon"), None),
        P(("band", "lon"), None),
        P(None, ("band", "lon"), None),
        P(("band", "lon"), None, None),
        P(("band", "lon"), None, None, None),
        P(("band", "lon"), None, None),
        P(("band", "lon"), None, None, None),
        P(("band", "lon"), None),
        P(("band", "lon"), None),
        P(("band", "lon"), None),
        P(("band", "lon")),
    )
    return jax.shard_map(
        on_device,
        mesh=mesh,
        in_specs=placed,
        out_specs=(P(None, ("band", "lon"), None), P(None, ("band", "lon"), None)),
        check_vma=False,
    )
```

```python
import math

import jax
import jax.numpy as jnp
from jax import lax
from jax.sharding import PartitionSpec as P

REACH = 6
ITERS = 2


MATMUL_PRECISION = lax.Precision.HIGH
ROOT_THREE = math.sqrt(3.0)
AMPLITUDE = 0.02


def extended(cells, sides, width):
    for axis, dim in sides:
        count = lax.axis_size(axis)
        head = lax.slice_in_dim(cells, 0, width, axis=dim)
        tail = lax.slice_in_dim(cells, cells.shape[dim] - width, cells.shape[dim], axis=dim)
        cells = jnp.concatenate(
            [
                lax.ppermute(tail, axis, [(i, (i + 1) % count) for i in range(count)]),
                cells,
                lax.ppermute(head, axis, [((i + 1) % count, i) for i in range(count)]),
            ],
            axis=dim,
        )
    return cells


def gathered(vector, axis):
    count = lax.axis_size(axis)
    copies = jnp.broadcast_to(vector[None], (count,) + vector.shape)
    return lax.all_to_all(copies, axis, 0, 0, tiled=False)


def all_sum(vector, axes):
    for axis in axes:
        vector = jnp.sum(gathered(vector, axis), axis=0)
    return vector


def matern_shape(rows_pos, cols_pos, length_scale):
    squared = None
    for component in range(3):
        offset = rows_pos[component][:, :, None] - cols_pos[component][:, None, :]
        squared = offset * offset if squared is None else squared + offset * offset
    scaled = jnp.sqrt(squared) * (ROOT_THREE / length_scale)
    return (1.0 + scaled) * jnp.exp(-scaled)


def on_device(
    sky_maps,
    noise_var,
    position,
    leaf_basis,
    leaf_couple,
    transfer,
    panel_couple,
    near_list,
    far_list,
    panel_list,
    leaf_panel,
):
    lon_index = lax.axis_index("lon")
    lon_count = lax.axis_size("lon")
    local_leaves = sky_maps.shape[1]
    pixel_count = sky_maps.shape[2]
    cycle_size = local_leaves * lon_count
    panel_count = panel_couple.shape[0]
    length_scale = 2.0 * math.pi / cycle_size
    first_leaf = lon_index * local_leaves
    near_depth = 2

    def rim_index(leaf_ids, depth):
        return (leaf_ids % cycle_size - first_leaf + depth) % cycle_size

    near_valid = near_list >= 0
    near_rows = rim_index(jnp.where(near_valid, near_list, near_list[:, :1]), near_depth)
    far_rows = rim_index(far_list, REACH)
    rim_pos = extended(position, (("lon", 1),), near_depth)

    same_blocks = matern_shape(
        rim_pos[:, near_depth : near_depth + local_leaves],
        rim_pos[:, near_depth : near_depth + local_leaves],
        length_scale,
    )
    step_blocks = [
        matern_shape(
            rim_pos[:, near_depth - step : near_depth + local_leaves],
            rim_pos[:, near_depth : near_depth + local_leaves + step],
            length_scale,
        )
        for step in range(1, near_depth + 1)
    ]
    step_range = jnp.arange(-near_depth, near_depth + 1, dtype=jnp.int32)
    targets = jnp.arange(local_leaves, dtype=jnp.int32)[:, None] + near_depth + step_range[None, :]
    matches = (near_rows[:, :, None] == targets[:, None, :]) & near_valid[:, :, None]
    offset_scale = AMPLITUDE * jnp.sum(matches.astype(jnp.float32), axis=1)
    band_slot = panel_list // (lon_count * panel_count)
    gathered_rows = band_slot * panel_count + panel_list % panel_count
    membership = (leaf_panel[:, None] == jnp.arange(panel_count, dtype=jnp.int32)[None, :]).astype(
        jnp.float32
    )

    def covariance_local(direction):
        coeffs = jnp.einsum("lpr,mlp->mlr", leaf_basis, direction, precision=MATMUL_PRECISION)
        joined = jnp.concatenate([direction, coeffs], axis=2)
        rim_joined = extended(joined, (("lon", 1),), REACH)
        rim_values = rim_joined[
            :, REACH - near_depth : REACH + local_leaves + near_depth, :pixel_count
        ]
        rim_coeffs = rim_joined[:, :, pixel_count:]

        def offset_values(step):
            start = near_depth + step
            values = rim_values[:, start : start + local_leaves]
            return values * offset_scale[None, :, step + near_depth, None]

        near_part = jnp.einsum(
            "ipq,miq->mip", same_blocks, offset_values(0), precision=MATMUL_PRECISION
        )
        for step in range(1, near_depth + 1):
            blocks = step_blocks[step - 1]
            ahead = blocks[step : step + local_leaves]
            behind = blocks[:local_leaves]
            near_part = near_part + jnp.einsum(
                "ipq,miq->mip", ahead, offset_values(step), precision=MATMUL_PRECISION
            )
            near_part = near_part + jnp.einsum(
                "iqp,miq->mip", behind, offset_values(-step), precision=MATMUL_PRECISION
            )
        leaf_far = jnp.einsum(
            "lsab,mlsb->mla", leaf_couple, rim_coeffs[:, far_rows], precision=MATMUL_PRECISION
        )
        upward = jnp.einsum("lab,mla->mlb", transfer, coeffs, precision=MATMUL_PRECISION)
        panel_coeffs = jnp.einsum("lk,mlb->mkb", membership, upward, precision=MATMUL_PRECISION)
        return direction, near_part, leaf_far, panel_coeffs

    def band_layout(band_panels, panel_coeffs):
        stacked = band_panels.reshape((band_panels.shape[0],) + panel_coeffs.shape)
        return jnp.swapaxes(stacked, 0, 1).reshape(
            panel_coeffs.shape[0], -1, panel_coeffs.shape[2]
        )

    def covariance_finish(local, band_coeffs):
        direction, near_part, leaf_far, panel_coeffs = local
        panel_far = jnp.einsum(
            "ksab,mksb->mka",
            panel_couple,
            band_coeffs[:, gathered_rows],
            precision=MATMUL_PRECISION,
        )
        downward = jnp.einsum("lk,mkb->mlb", membership, panel_far, precision=MATMUL_PRECISION)
        leaf_far = leaf_far + jnp.einsum(
            "lab,mlb->mla", transfer, downward, precision=MATMUL_PRECISION
        )
        far_part = jnp.einsum("lpr,mlr->mlp", leaf_basis, leaf_far, precision=MATMUL_PRECISION)
        return noise_var[None] * direction + near_part + far_part

    def covariance_apply(direction):
        local = covariance_local(direction)
        panel_coeffs = local[3]
        band_panels = gathered(panel_coeffs.reshape(-1), "band")
        return covariance_finish(local, band_layout(band_panels, panel_coeffs))

    def total(*products):
        sums = jnp.stack([jnp.sum(product, axis=(1, 2)) for product in products])
        return all_sum(sums, ("lon", "band"))

    assert ITERS == 2
    direction = sky_maps
    applied = covariance_apply(direction)
    applied_local = covariance_local(applied)
    first_sums = jnp.stack(
        [jnp.sum(product, axis=(1, 2)) for product in (direction * direction, direction * applied)]
    )
    first_sums = all_sum(first_sums, ("lon",))
    panel_coeffs = applied_local[3]
    payload = jnp.concatenate([panel_coeffs.reshape(-1), first_sums.reshape(-1)])
    band_payload = gathered(payload, "band")
    panel_size = panel_coeffs.size
    norm_now, curvature_sum = jnp.sum(band_payload[:, panel_size:], axis=0).reshape(
        first_sums.shape
    )
    applied_twice = covariance_finish(
        applied_local, band_layout(band_payload[:, :panel_size], panel_coeffs)
    )
    step_size = (norm_now / curvature_sum)[:, None, None]
    solution = step_size * direction
    residual = direction - step_size * applied
    applied_residual = applied - step_size * applied_twice
    norm_next, residual_curv, cross_one, cross_two = total(
        residual * residual,
        residual * applied_residual,
        residual * applied,
        direction * applied_residual,
    )
    ratio = norm_next / norm_now
    next_curv = residual_curv + ratio * (cross_one + cross_two) + ratio * ratio * curvature_sum
    ratio = ratio[:, None, None]
    step_next = (norm_next / next_curv)[:, None, None]
    solution = solution + step_next * (residual + ratio * direction)
    residual = residual - step_next * (applied_residual + ratio * applied)
    return (solution, residual)


def solution(mesh):
    placed = (
        P(None, ("band", "lon"), None),
        P(("band", "lon"), None),
        P(None, ("band", "lon"), None),
        P(("band", "lon"), None, None),
        P(("band", "lon"), None, None, None),
        P(("band", "lon"), None, None),
        P(("band", "lon"), None, None, None),
        P(("band", "lon"), None),
        P(("band", "lon"), None),
        P(("band", "lon"), None),
        P(("band", "lon")),
    )
    return jax.shard_map(
        on_device,
        mesh=mesh,
        in_specs=placed,
        out_specs=(P(None, ("band", "lon"), None), P(None, ("band", "lon"), None)),
        check_vma=False,
    )
```

```python
import math

import jax
import jax.numpy as jnp
from jax import lax
from jax.sharding import PartitionSpec as P

REACH = 6
ITERS = 2


MATMUL_PRECISION = lax.Precision.HIGH
ROOT_THREE = math.sqrt(3.0)
AMPLITUDE = 0.02


def extended(cells, sides, width):
    for axis, dim in sides:
        count = lax.axis_size(axis)
        head = lax.slice_in_dim(cells, 0, width, axis=dim)
        tail = lax.slice_in_dim(cells, cells.shape[dim] - width, cells.shape[dim], axis=dim)
        cells = jnp.concatenate(
            [
                lax.ppermute(tail, axis, [(i, (i + 1) % count) for i in range(count)]),
                cells,
                lax.ppermute(head, axis, [((i + 1) % count, i) for i in range(count)]),
            ],
            axis=dim,
        )
    return cells


def gathered(vector, axis):
    count = lax.axis_size(axis)
    copies = jnp.broadcast_to(vector[None], (count,) + vector.shape)
    return lax.all_to_all(copies, axis, 0, 0, tiled=False)


def all_sum(vector, axes):
    for axis in axes:
        vector = jnp.sum(gathered(vector, axis), axis=0)
    return vector


def matern_shape(rows_pos, cols_pos, length_scale):
    squared = None
    for component in range(3):
        offset = rows_pos[component][:, :, None] - cols_pos[component][:, None, :]
        squared = offset * offset if squared is None else squared + offset * offset
    scaled = jnp.sqrt(squared) * (ROOT_THREE / length_scale)
    return (1.0 + scaled) * jnp.exp(-scaled)


def on_device(
    sky_maps,
    noise_var,
    position,
    leaf_basis,
    leaf_couple,
    transfer,
    panel_couple,
    near_list,
    far_list,
    panel_list,
    leaf_panel,
):
    lon_index = lax.axis_index("lon")
    lon_count = lax.axis_size("lon")
    local_leaves = sky_maps.shape[1]
    pixel_count = sky_maps.shape[2]
    cycle_size = local_leaves * lon_count
    panel_count = panel_couple.shape[0]
    length_scale = 2.0 * math.pi / cycle_size
    first_leaf = lon_index * local_leaves
    near_depth = 2

    def rim_index(leaf_ids, depth):
        return (leaf_ids % cycle_size - first_leaf + depth) % cycle_size

    near_valid = near_list >= 0
    near_rows = rim_index(jnp.where(near_valid, near_list, near_list[:, :1]), near_depth)
    far_rows = rim_index(far_list, REACH)
    rim_pos = extended(position, (("lon", 1),), near_depth)

    same_blocks = matern_shape(
        rim_pos[:, near_depth : near_depth + local_leaves],
        rim_pos[:, near_depth : near_depth + local_leaves],
        length_scale,
    )
    step_blocks = [
        matern_shape(
            rim_pos[:, near_depth - step : near_depth + local_leaves],
            rim_pos[:, near_depth : near_depth + local_leaves + step],
            length_scale,
        )
        for step in range(1, near_depth + 1)
    ]
    step_range = jnp.arange(-near_depth, near_depth + 1, dtype=jnp.int32)
    targets = jnp.arange(local_leaves, dtype=jnp.int32)[:, None] + near_depth + step_range[None, :]
    matches = (near_rows[:, :, None] == targets[:, None, :]) & near_valid[:, :, None]
    offset_scale = AMPLITUDE * jnp.sum(matches.astype(jnp.float32), axis=1)
    band_slot = panel_list // (lon_count * panel_count)
    gathered_rows = band_slot * panel_count + panel_list % panel_count
    membership = (leaf_panel[:, None] == jnp.arange(panel_count, dtype=jnp.int32)[None, :]).astype(
        jnp.float32
    )

    def covariance_local(direction):
        coeffs = jnp.einsum("lpr,mlp->mlr", leaf_basis, direction, precision=MATMUL_PRECISION)
        joined = jnp.concatenate([direction, coeffs], axis=2)
        rim_joined = extended(joined, (("lon", 1),), REACH)
        rim_values = rim_joined[
            :, REACH - near_depth : REACH + local_leaves + near_depth, :pixel_count
        ]
        rim_coeffs = rim_joined[:, :, pixel_count:]

        def offset_values(step):
            start = near_depth + step
            values = rim_values[:, start : start + local_leaves]
            return values * offset_scale[None, :, step + near_depth, None]

        near_part = jnp.einsum(
            "ipq,miq->mip", same_blocks, offset_values(0), precision=MATMUL_PRECISION
        )
        for step in range(1, near_depth + 1):
            blocks = step_blocks[step - 1]
            ahead = blocks[step : step + local_leaves]
            behind = blocks[:local_leaves]
            near_part = near_part + jnp.einsum(
                "ipq,miq->mip", ahead, offset_values(step), precision=MATMUL_PRECISION
            )
            near_part = near_part + jnp.einsum(
                "iqp,miq->mip", behind, offset_values(-step), precision=MATMUL_PRECISION
            )
        leaf_far = jnp.einsum(
            "lsab,mlsb->mla", leaf_couple, rim_coeffs[:, far_rows], precision=MATMUL_PRECISION
        )
        upward = jnp.einsum("lab,mla->mlb", transfer, coeffs, precision=MATMUL_PRECISION)
        panel_coeffs = jnp.einsum("lk,mlb->mkb", membership, upward, precision=MATMUL_PRECISION)
        return direction, near_part, leaf_far, panel_coeffs

    def band_layout(band_panels, panel_coeffs):
        stacked = band_panels.reshape((band_panels.shape[0],) + panel_coeffs.shape)
        return jnp.swapaxes(stacked, 0, 1).reshape(
            panel_coeffs.shape[0], -1, panel_coeffs.shape[2]
        )

    def covariance_finish(local, band_coeffs):
        direction, near_part, leaf_far, panel_coeffs = local
        panel_far = jnp.einsum(
            "ksab,mksb->mka",
            panel_couple,
            band_coeffs[:, gathered_rows],
            precision=MATMUL_PRECISION,
        )
        downward = jnp.einsum("lk,mkb->mlb", membership, panel_far, precision=MATMUL_PRECISION)
        leaf_far = leaf_far + jnp.einsum(
            "lab,mlb->mla", transfer, downward, precision=MATMUL_PRECISION
        )
        far_part = jnp.einsum("lpr,mlr->mlp", leaf_basis, leaf_far, precision=MATMUL_PRECISION)
        return noise_var[None] * direction + near_part + far_part

    def covariance_apply(direction):
        local = covariance_local(direction)
        panel_coeffs = local[3]
        _, panel_coeffs = lax.optimization_barrier(((same_blocks, step_blocks), panel_coeffs))
        band_panels = gathered(panel_coeffs.reshape(-1), "band")
        return covariance_finish(local, band_layout(band_panels, panel_coeffs))

    def total(*products):
        sums = jnp.stack([jnp.sum(product, axis=(1, 2)) for product in products])
        return all_sum(sums, ("lon", "band"))

    assert ITERS == 2
    direction = sky_maps
    applied = covariance_apply(direction)
    applied_local = covariance_local(applied)
    first_sums = jnp.stack(
        [jnp.sum(product, axis=(1, 2)) for product in (direction * direction, direction * applied)]
    )
    first_sums = all_sum(first_sums, ("lon",))
    panel_coeffs = applied_local[3]
    payload = jnp.concatenate([panel_coeffs.reshape(-1), first_sums.reshape(-1)])
    band_payload = gathered(payload, "band")
    panel_size = panel_coeffs.size
    norm_now, curvature_sum = jnp.sum(band_payload[:, panel_size:], axis=0).reshape(
        first_sums.shape
    )
    applied_twice = covariance_finish(
        applied_local, band_layout(band_payload[:, :panel_size], panel_coeffs)
    )
    step_size = (norm_now / curvature_sum)[:, None, None]
    solution = step_size * direction
    residual = direction - step_size * applied
    applied_residual = applied - step_size * applied_twice
    norm_next, residual_curv, cross_one, cross_two = total(
        residual * residual,
        residual * applied_residual,
        residual * applied,
        direction * applied_residual,
    )
    ratio = norm_next / norm_now
    next_curv = residual_curv + ratio * (cross_one + cross_two) + ratio * ratio * curvature_sum
    ratio = ratio[:, None, None]
    step_next = (norm_next / next_curv)[:, None, None]
    solution = solution + step_next * (residual + ratio * direction)
    residual = residual - step_next * (applied_residual + ratio * applied)
    return (solution, residual)


def solution(mesh):
    placed = (
        P(None, ("band", "lon"), None),
        P(("band", "lon"), None),
        P(None, ("band", "lon"), None),
        P(("band", "lon"), None, None),
        P(("band", "lon"), None, None, None),
        P(("band", "lon"), None, None),
        P(("band", "lon"), None, None, None),
        P(("band", "lon"), None),
        P(("band", "lon"), None),
        P(("band", "lon"), None),
        P(("band", "lon")),
    )
    return jax.shard_map(
        on_device,
        mesh=mesh,
        in_specs=placed,
        out_specs=(P(None, ("band", "lon"), None), P(None, ("band", "lon"), None)),
        check_vma=False,
    )
```

```python
import math

import jax
import jax.numpy as jnp
from jax import lax
from jax.sharding import PartitionSpec as P

REACH = 6
ITERS = 2


MATMUL_PRECISION = lax.Precision.HIGH
ROOT_THREE = math.sqrt(3.0)
AMPLITUDE = 0.02


def extended(cells, sides, width):
    for axis, dim in sides:
        count = lax.axis_size(axis)
        head = lax.slice_in_dim(cells, 0, width, axis=dim)
        tail = lax.slice_in_dim(cells, cells.shape[dim] - width, cells.shape[dim], axis=dim)
        cells = jnp.concatenate(
            [
                lax.ppermute(tail, axis, [(i, (i + 1) % count) for i in range(count)]),
                cells,
                lax.ppermute(head, axis, [((i + 1) % count, i) for i in range(count)]),
            ],
            axis=dim,
        )
    return cells


def gathered(vector, axis):
    count = lax.axis_size(axis)
    copies = jnp.broadcast_to(vector[None], (count,) + vector.shape)
    return lax.all_to_all(copies, axis, 0, 0, tiled=False)


def all_sum(vector, axes):
    for axis in axes:
        vector = jnp.sum(gathered(vector, axis), axis=0)
    return vector


def matern_shape(rows_pos, cols_pos, length_scale):
    squared = None
    for component in range(3):
        offset = rows_pos[component][:, :, None] - cols_pos[component][:, None, :]
        squared = offset * offset if squared is None else squared + offset * offset
    scaled = jnp.sqrt(squared) * (ROOT_THREE / length_scale)
    return (1.0 + scaled) * jnp.exp(-scaled)


def on_device(
    sky_maps,
    noise_var,
    position,
    leaf_basis,
    leaf_couple,
    transfer,
    panel_couple,
    near_list,
    far_list,
    panel_list,
    leaf_panel,
):
    lon_index = lax.axis_index("lon")
    lon_count = lax.axis_size("lon")
    local_leaves = sky_maps.shape[1]
    pixel_count = sky_maps.shape[2]
    cycle_size = local_leaves * lon_count
    panel_count = panel_couple.shape[0]
    length_scale = 2.0 * math.pi / cycle_size
    first_leaf = lon_index * local_leaves
    near_depth = 2

    def rim_index(leaf_ids, depth):
        return (leaf_ids % cycle_size - first_leaf + depth) % cycle_size

    near_valid = near_list >= 0
    near_rows = rim_index(jnp.where(near_valid, near_list, near_list[:, :1]), near_depth)
    far_rows = rim_index(far_list, REACH)
    rim_pos = extended(position, (("lon", 1),), near_depth)

    same_blocks = matern_shape(
        rim_pos[:, near_depth : near_depth + local_leaves],
        rim_pos[:, near_depth : near_depth + local_leaves],
        length_scale,
    )
    step_blocks = [
        matern_shape(
            rim_pos[:, near_depth - step : near_depth + local_leaves],
            rim_pos[:, near_depth : near_depth + local_leaves + step],
            length_scale,
        )
        for step in range(1, near_depth + 1)
    ]
    step_range = jnp.arange(-near_depth, near_depth + 1, dtype=jnp.int32)
    targets = jnp.arange(local_leaves, dtype=jnp.int32)[:, None] + near_depth + step_range[None, :]
    matches = (near_rows[:, :, None] == targets[:, None, :]) & near_valid[:, :, None]
    offset_scale = AMPLITUDE * jnp.sum(matches.astype(jnp.float32), axis=1)
    band_slot = panel_list // (lon_count * panel_count)
    gathered_rows = band_slot * panel_count + panel_list % panel_count
    membership = (leaf_panel[:, None] == jnp.arange(panel_count, dtype=jnp.int32)[None, :]).astype(
        jnp.float32
    )

    def covariance_local(direction):
        coeffs = jnp.einsum("lpr,mlp->mlr", leaf_basis, direction, precision=MATMUL_PRECISION)
        joined = jnp.concatenate([direction, coeffs], axis=2)
        rim_joined = extended(joined, (("lon", 1),), REACH)
        rim_values = rim_joined[
            :, REACH - near_depth : REACH + local_leaves + near_depth, :pixel_count
        ]
        rim_coeffs = rim_joined[:, :, pixel_count:]

        def offset_values(step):
            start = near_depth + step
            values = rim_values[:, start : start + local_leaves]
            return values * offset_scale[None, :, step + near_depth, None]

        near_part = jnp.einsum(
            "ipq,miq->mip", same_blocks, offset_values(0), precision=MATMUL_PRECISION
        )
        for step in range(1, near_depth + 1):
            blocks = step_blocks[step - 1]
            ahead = blocks[step : step + local_leaves]
            behind = blocks[:local_leaves]
            near_part = near_part + jnp.einsum(
                "ipq,miq->mip", ahead, offset_values(step), precision=MATMUL_PRECISION
            )
            near_part = near_part + jnp.einsum(
                "iqp,miq->mip", behind, offset_values(-step), precision=MATMUL_PRECISION
            )
        leaf_far = jnp.einsum(
            "lsab,mlsb->mla", leaf_couple, rim_coeffs[:, far_rows], precision=MATMUL_PRECISION
        )
        upward = jnp.einsum("lab,mla->mlb", transfer, coeffs, precision=MATMUL_PRECISION)
        panel_coeffs = jnp.einsum("lk,mlb->mkb", membership, upward, precision=MATMUL_PRECISION)
        return direction, near_part, leaf_far, panel_coeffs

    def band_layout(band_panels, panel_coeffs):
        stacked = band_panels.reshape((band_panels.shape[0],) + panel_coeffs.shape)
        return jnp.swapaxes(stacked, 0, 1).reshape(
            panel_coeffs.shape[0], -1, panel_coeffs.shape[2]
        )

    def covariance_finish(local, band_coeffs):
        direction, near_part, leaf_far, panel_coeffs = local
        panel_far = jnp.einsum(
            "ksab,mksb->mka",
            panel_couple,
            band_coeffs[:, gathered_rows],
            precision=MATMUL_PRECISION,
        )
        downward = jnp.einsum("lk,mkb->mlb", membership, panel_far, precision=MATMUL_PRECISION)
        leaf_far = leaf_far + jnp.einsum(
            "lab,mlb->mla", transfer, downward, precision=MATMUL_PRECISION
        )
        far_part = jnp.einsum("lpr,mlr->mlp", leaf_basis, leaf_far, precision=MATMUL_PRECISION)
        return noise_var[None] * direction + near_part + far_part

    def covariance_apply(direction):
        local = covariance_local(direction)
        panel_coeffs = local[3]
        band_panels = gathered(panel_coeffs.reshape(-1), "band")
        return covariance_finish(local, band_layout(band_panels, panel_coeffs))

    def total(*products):
        sums = jnp.stack([jnp.sum(product, axis=(1, 2)) for product in products])
        return all_sum(sums, ("band", "lon"))

    assert ITERS == 2
    direction = sky_maps
    applied = covariance_apply(direction)
    applied_local = covariance_local(applied)
    first_sums = jnp.stack(
        [jnp.sum(product, axis=(1, 2)) for product in (direction * direction, direction * applied)]
    )
    first_sums = all_sum(first_sums, ("lon",))
    panel_coeffs = applied_local[3]
    payload = jnp.concatenate([panel_coeffs.reshape(-1), first_sums.reshape(-1)])
    band_payload = gathered(payload, "band")
    panel_size = panel_coeffs.size
    norm_now, curvature_sum = jnp.sum(band_payload[:, panel_size:], axis=0).reshape(
        first_sums.shape
    )
    applied_twice = covariance_finish(
        applied_local, band_layout(band_payload[:, :panel_size], panel_coeffs)
    )
    step_size = (norm_now / curvature_sum)[:, None, None]
    solution = step_size * direction
    residual = direction - step_size * applied
    applied_residual = applied - step_size * applied_twice
    norm_next, residual_curv, cross_one, cross_two = total(
        residual * residual,
        residual * applied_residual,
        residual * applied,
        direction * applied_residual,
    )
    ratio = norm_next / norm_now
    next_curv = residual_curv + ratio * (cross_one + cross_two) + ratio * ratio * curvature_sum
    ratio = ratio[:, None, None]
    step_next = (norm_next / next_curv)[:, None, None]
    solution = solution + step_next * (residual + ratio * direction)
    residual = residual - step_next * (applied_residual + ratio * applied)
    return (solution, residual)


def solution(mesh):
    placed = (
        P(None, ("band", "lon"), None),
        P(("band", "lon"), None),
        P(None, ("band", "lon"), None),
        P(("band", "lon"), None, None),
        P(("band", "lon"), None, None, None),
        P(("band", "lon"), None, None),
        P(("band", "lon"), None, None, None),
        P(("band", "lon"), None),
        P(("band", "lon"), None),
        P(("band", "lon"), None),
        P(("band", "lon")),
    )
    return jax.shard_map(
        on_device,
        mesh=mesh,
        in_specs=placed,
        out_specs=(P(None, ("band", "lon"), None), P(None, ("band", "lon"), None)),
        check_vma=False,
    )
```

```python
import math

import jax
import jax.numpy as jnp
from jax import lax
from jax.sharding import PartitionSpec as P

REACH = 6
ITERS = 2


MATMUL_PRECISION = lax.Precision.HIGH
ROOT_THREE = math.sqrt(3.0)
AMPLITUDE = 0.02


def extended(cells, sides, width):
    for axis, dim in sides:
        count = lax.axis_size(axis)
        head = lax.slice_in_dim(cells, 0, width, axis=dim)
        tail = lax.slice_in_dim(cells, cells.shape[dim] - width, cells.shape[dim], axis=dim)
        cells = jnp.concatenate(
            [
                lax.ppermute(tail, axis, [(i, (i + 1) % count) for i in range(count)]),
                cells,
                lax.ppermute(head, axis, [((i + 1) % count, i) for i in range(count)]),
            ],
            axis=dim,
        )
    return cells


def gathered(vector, axis):
    count = lax.axis_size(axis)
    copies = jnp.broadcast_to(vector[None], (count,) + vector.shape)
    return lax.all_to_all(copies, axis, 0, 0, tiled=False)


def all_sum(vector, axes):
    for axis in axes:
        vector = jnp.sum(gathered(vector, axis), axis=0)
    return vector


def matern_shape(rows_pos, cols_pos, length_scale):
    squared = None
    for component in range(3):
        offset = rows_pos[component][:, :, None] - cols_pos[component][:, None, :]
        squared = offset * offset if squared is None else squared + offset * offset
    scaled = jnp.sqrt(squared) * (ROOT_THREE / length_scale)
    return (1.0 + scaled) * jnp.exp(-scaled)


def on_device(
    sky_maps,
    noise_var,
    position,
    leaf_basis,
    leaf_couple,
    transfer,
    panel_couple,
    near_list,
    far_list,
    panel_list,
    leaf_panel,
):
    lon_index = lax.axis_index("lon")
    lon_count = lax.axis_size("lon")
    local_leaves = sky_maps.shape[1]
    pixel_count = sky_maps.shape[2]
    cycle_size = local_leaves * lon_count
    panel_count = panel_couple.shape[0]
    length_scale = 2.0 * math.pi / cycle_size
    first_leaf = lon_index * local_leaves
    near_depth = 2

    def rim_index(leaf_ids, depth):
        return (leaf_ids % cycle_size - first_leaf + depth) % cycle_size

    near_valid = near_list >= 0
    near_rows = rim_index(jnp.where(near_valid, near_list, near_list[:, :1]), near_depth)
    far_rows = rim_index(far_list, REACH)
    rim_pos = extended(position, (("lon", 1),), near_depth)

    same_blocks = matern_shape(
        rim_pos[:, near_depth : near_depth + local_leaves],
        rim_pos[:, near_depth : near_depth + local_leaves],
        length_scale,
    )
    step_blocks = [
        matern_shape(
            rim_pos[:, near_depth - step : near_depth + local_leaves],
            rim_pos[:, near_depth : near_depth + local_leaves + step],
            length_scale,
        )
        for step in range(1, near_depth + 1)
    ]
    step_range = jnp.arange(-near_depth, near_depth + 1, dtype=jnp.int32)
    targets = jnp.arange(local_leaves, dtype=jnp.int32)[:, None] + near_depth + step_range[None, :]
    matches = (near_rows[:, :, None] == targets[:, None, :]) & near_valid[:, :, None]
    offset_scale = AMPLITUDE * jnp.sum(matches.astype(jnp.float32), axis=1)
    band_slot = panel_list // (lon_count * panel_count)
    gathered_rows = band_slot * panel_count + panel_list % panel_count
    membership = (leaf_panel[:, None] == jnp.arange(panel_count, dtype=jnp.int32)[None, :]).astype(
        jnp.float32
    )

    def covariance_local(direction):
        coeffs = jnp.einsum("lpr,mlp->mlr", leaf_basis, direction, precision=MATMUL_PRECISION)
        joined = jnp.concatenate([direction, coeffs], axis=2)
        rim_joined = extended(joined, (("lon", 1),), REACH)
        rim_values = rim_joined[
            :, REACH - near_depth : REACH + local_leaves + near_depth, :pixel_count
        ]
        rim_coeffs = rim_joined[:, :, pixel_count:]

        def offset_values(step):
            start = near_depth + step
            values = rim_values[:, start : start + local_leaves]
            return values * offset_scale[None, :, step + near_depth, None]

        near_part = jnp.einsum(
            "ipq,miq->mip", same_blocks, offset_values(0), precision=MATMUL_PRECISION
        )
        for step in range(1, near_depth + 1):
            blocks = step_blocks[step - 1]
            ahead = blocks[step : step + local_leaves]
            behind = blocks[:local_leaves]
            near_part = near_part + jnp.einsum(
                "ipq,miq->mip", ahead, offset_values(step), precision=MATMUL_PRECISION
            )
            near_part = near_part + jnp.einsum(
                "iqp,miq->mip", behind, offset_values(-step), precision=MATMUL_PRECISION
            )
        leaf_far = jnp.einsum(
            "lsab,mlsb->mla", leaf_couple, rim_coeffs[:, far_rows], precision=MATMUL_PRECISION
        )
        upward = jnp.einsum("lab,mla->mlb", transfer, coeffs, precision=MATMUL_PRECISION)
        panel_coeffs = jnp.einsum("lk,mlb->mkb", membership, upward, precision=MATMUL_PRECISION)
        return direction, near_part, leaf_far, panel_coeffs

    def band_layout(band_panels, panel_coeffs):
        stacked = band_panels.reshape((band_panels.shape[0],) + panel_coeffs.shape)
        return jnp.swapaxes(stacked, 0, 1).reshape(
            panel_coeffs.shape[0], -1, panel_coeffs.shape[2]
        )

    def covariance_finish(local, band_coeffs):
        direction, near_part, leaf_far, panel_coeffs = local
        panel_far = jnp.einsum(
            "ksab,mksb->mka",
            panel_couple,
            band_coeffs[:, gathered_rows],
            precision=MATMUL_PRECISION,
        )
        downward = jnp.einsum("lk,mkb->mlb", membership, panel_far, precision=MATMUL_PRECISION)
        leaf_far = leaf_far + jnp.einsum(
            "lab,mlb->mla", transfer, downward, precision=MATMUL_PRECISION
        )
        far_part = jnp.einsum("lpr,mlr->mlp", leaf_basis, leaf_far, precision=MATMUL_PRECISION)
        return noise_var[None] * direction + near_part + far_part

    def covariance_apply(direction):
        local = covariance_local(direction)
        panel_coeffs = local[3]
        band_panels = gathered(panel_coeffs.reshape(-1), "band")
        return covariance_finish(local, band_layout(band_panels, panel_coeffs))

    def total(*products):
        sums = jnp.stack([jnp.sum(product, axis=(1, 2)) for product in products])
        return all_sum(sums, ("lon", "band"))

    assert ITERS == 2
    direction = sky_maps
    applied = covariance_apply(direction)
    applied_local = covariance_local(applied)
    first_sums = jnp.stack(
        [jnp.sum(product, axis=(1, 2)) for product in (direction * direction, direction * applied)]
    )
    panel_coeffs = applied_local[3]
    payload = jnp.concatenate([panel_coeffs.reshape(-1), first_sums.reshape(-1)])
    band_payload = gathered(payload, "band")
    panel_size = panel_coeffs.size
    first_sums = jnp.sum(band_payload[:, panel_size:], axis=0).reshape(first_sums.shape)
    norm_now, curvature_sum = all_sum(first_sums, ("lon",))
    applied_twice = covariance_finish(
        applied_local, band_layout(band_payload[:, :panel_size], panel_coeffs)
    )
    step_size = (norm_now / curvature_sum)[:, None, None]
    solution = step_size * direction
    residual = direction - step_size * applied
    applied_residual = applied - step_size * applied_twice
    norm_next, residual_curv, cross_one, cross_two = total(
        residual * residual,
        residual * applied_residual,
        residual * applied,
        direction * applied_residual,
    )
    ratio = norm_next / norm_now
    next_curv = residual_curv + ratio * (cross_one + cross_two) + ratio * ratio * curvature_sum
    ratio = ratio[:, None, None]
    step_next = (norm_next / next_curv)[:, None, None]
    solution = solution + step_next * (residual + ratio * direction)
    residual = residual - step_next * (applied_residual + ratio * applied)
    return (solution, residual)


def solution(mesh):
    placed = (
        P(None, ("band", "lon"), None),
        P(("band", "lon"), None),
        P(None, ("band", "lon"), None),
        P(("band", "lon"), None, None),
        P(("band", "lon"), None, None, None),
        P(("band", "lon"), None, None),
        P(("band", "lon"), None, None, None),
        P(("band", "lon"), None),
        P(("band", "lon"), None),
        P(("band", "lon"), None),
        P(("band", "lon")),
    )
    return jax.shard_map(
        on_device,
        mesh=mesh,
        in_specs=placed,
        out_specs=(P(None, ("band", "lon"), None), P(None, ("band", "lon"), None)),
        check_vma=False,
    )
```

```python
import math

import jax
import jax.numpy as jnp
from jax import lax
from jax.sharding import PartitionSpec as P

REACH = 6
ITERS = 2


MATMUL_PRECISION = lax.Precision.HIGH
ROOT_THREE = math.sqrt(3.0)
AMPLITUDE = 0.02


def extended(cells, sides, width):
    for axis, dim in sides:
        count = lax.axis_size(axis)
        head = lax.slice_in_dim(cells, 0, width, axis=dim)
        tail = lax.slice_in_dim(cells, cells.shape[dim] - width, cells.shape[dim], axis=dim)
        cells = jnp.concatenate(
            [
                lax.ppermute(tail, axis, [(i, (i + 1) % count) for i in range(count)]),
                cells,
                lax.ppermute(head, axis, [((i + 1) % count, i) for i in range(count)]),
            ],
            axis=dim,
        )
    return cells


def gathered(vector, axis):
    count = lax.axis_size(axis)
    copies = jnp.broadcast_to(vector[None], (count,) + vector.shape)
    return lax.all_to_all(copies, axis, 0, 0, tiled=False)


def all_sum(vector, axes):
    for axis in axes:
        vector = jnp.sum(gathered(vector, axis), axis=0)
    return vector


def matern_shape(rows_pos, cols_pos, length_scale):
    squared = None
    for component in range(3):
        offset = rows_pos[component][:, :, None] - cols_pos[component][:, None, :]
        squared = offset * offset if squared is None else squared + offset * offset
    scaled = jnp.sqrt(squared) * (ROOT_THREE / length_scale)
    return (1.0 + scaled) * jnp.exp(-scaled)


def on_device(
    sky_maps,
    noise_var,
    position,
    leaf_basis,
    leaf_couple,
    transfer,
    panel_couple,
    near_list,
    far_list,
    panel_list,
    leaf_panel,
):
    lon_index = lax.axis_index("lon")
    lon_count = lax.axis_size("lon")
    local_leaves = sky_maps.shape[1]
    pixel_count = sky_maps.shape[2]
    cycle_size = local_leaves * lon_count
    panel_count = panel_couple.shape[0]
    length_scale = 2.0 * math.pi / cycle_size
    first_leaf = lon_index * local_leaves
    near_depth = 2

    def rim_index(leaf_ids, depth):
        return (leaf_ids % cycle_size - first_leaf + depth) % cycle_size

    near_valid = near_list >= 0
    near_rows = rim_index(jnp.where(near_valid, near_list, near_list[:, :1]), near_depth)
    far_rows = rim_index(far_list, REACH)
    rim_pos = extended(position, (("lon", 1),), near_depth)

    same_blocks = matern_shape(
        rim_pos[:, near_depth : near_depth + local_leaves],
        rim_pos[:, near_depth : near_depth + local_leaves],
        length_scale,
    )
    step_blocks = [
        matern_shape(
            rim_pos[:, near_depth - step : near_depth + local_leaves],
            rim_pos[:, near_depth : near_depth + local_leaves + step],
            length_scale,
        )
        for step in range(1, near_depth + 1)
    ]
    step_range = jnp.arange(-near_depth, near_depth + 1, dtype=jnp.int32)
    targets = jnp.arange(local_leaves, dtype=jnp.int32)[:, None] + near_depth + step_range[None, :]
    matches = (near_rows[:, :, None] == targets[:, None, :]) & near_valid[:, :, None]
    offset_scale = AMPLITUDE * jnp.sum(matches.astype(jnp.float32), axis=1)
    band_slot = panel_list // (lon_count * panel_count)
    gathered_rows = band_slot * panel_count + panel_list % panel_count
    membership = (leaf_panel[:, None] == jnp.arange(panel_count, dtype=jnp.int32)[None, :]).astype(
        jnp.float32
    )

    def covariance_local(direction):
        coeffs = jnp.einsum("lpr,mlp->mlr", leaf_basis, direction, precision=MATMUL_PRECISION)
        joined = jnp.concatenate([direction, coeffs], axis=2)
        rim_joined = extended(joined, (("lon", 1),), REACH)
        rim_values = rim_joined[
            :, REACH - near_depth : REACH + local_leaves + near_depth, :pixel_count
        ]
        rim_coeffs = rim_joined[:, :, pixel_count:]

        def offset_values(step):
            start = near_depth + step
            values = rim_values[:, start : start + local_leaves]
            return values * offset_scale[None, :, step + near_depth, None]

        near_part = jnp.einsum(
            "ipq,miq->mip", same_blocks, offset_values(0), precision=MATMUL_PRECISION
        )
        for step in range(1, near_depth + 1):
            blocks = step_blocks[step - 1]
            ahead = blocks[step : step + local_leaves]
            behind = blocks[:local_leaves]
            near_part = near_part + jnp.einsum(
                "ipq,miq->mip", ahead, offset_values(step), precision=MATMUL_PRECISION
            )
            near_part = near_part + jnp.einsum(
                "iqp,miq->mip", behind, offset_values(-step), precision=MATMUL_PRECISION
            )
        leaf_far = jnp.einsum(
            "lsab,mlsb->mla", leaf_couple, rim_coeffs[:, far_rows], precision=MATMUL_PRECISION
        )
        upward = jnp.einsum("lab,mla->mlb", transfer, coeffs, precision=MATMUL_PRECISION)
        panel_coeffs = jnp.sum(membership[None, :, :, None] * upward[:, :, None, :], axis=1)
        return direction, near_part, leaf_far, panel_coeffs

    def band_layout(band_panels, panel_coeffs):
        stacked = band_panels.reshape((band_panels.shape[0],) + panel_coeffs.shape)
        return jnp.swapaxes(stacked, 0, 1).reshape(
            panel_coeffs.shape[0], -1, panel_coeffs.shape[2]
        )

    def covariance_finish(local, band_coeffs):
        direction, near_part, leaf_far, panel_coeffs = local
        panel_far = jnp.einsum(
            "ksab,mksb->mka",
            panel_couple,
            band_coeffs[:, gathered_rows],
            precision=MATMUL_PRECISION,
        )
        downward = jnp.sum(membership[None, :, :, None] * panel_far[:, None, :, :], axis=2)
        leaf_far = leaf_far + jnp.einsum(
            "lab,mlb->mla", transfer, downward, precision=MATMUL_PRECISION
        )
        far_part = jnp.einsum("lpr,mlr->mlp", leaf_basis, leaf_far, precision=MATMUL_PRECISION)
        return noise_var[None] * direction + near_part + far_part

    def covariance_apply(direction):
        local = covariance_local(direction)
        panel_coeffs = local[3]
        band_panels = gathered(panel_coeffs.reshape(-1), "band")
        return covariance_finish(local, band_layout(band_panels, panel_coeffs))

    def total(*products):
        sums = jnp.stack([jnp.sum(product, axis=(1, 2)) for product in products])
        return all_sum(sums, ("lon", "band"))

    assert ITERS == 2
    direction = sky_maps
    applied = covariance_apply(direction)
    applied_local = covariance_local(applied)
    first_sums = jnp.stack(
        [jnp.sum(product, axis=(1, 2)) for product in (direction * direction, direction * applied)]
    )
    first_sums = all_sum(first_sums, ("lon",))
    panel_coeffs = applied_local[3]
    payload = jnp.concatenate([panel_coeffs.reshape(-1), first_sums.reshape(-1)])
    band_payload = gathered(payload, "band")
    panel_size = panel_coeffs.size
    norm_now, curvature_sum = jnp.sum(band_payload[:, panel_size:], axis=0).reshape(
        first_sums.shape
    )
    applied_twice = covariance_finish(
        applied_local, band_layout(band_payload[:, :panel_size], panel_coeffs)
    )
    step_size = (norm_now / curvature_sum)[:, None, None]
    solution = step_size * direction
    residual = direction - step_size * applied
    applied_residual = applied - step_size * applied_twice
    norm_next, residual_curv, cross_one, cross_two = total(
        residual * residual,
        residual * applied_residual,
        residual * applied,
        direction * applied_residual,
    )
    ratio = norm_next / norm_now
    next_curv = residual_curv + ratio * (cross_one + cross_two) + ratio * ratio * curvature_sum
    ratio = ratio[:, None, None]
    step_next = (norm_next / next_curv)[:, None, None]
    solution = solution + step_next * (residual + ratio * direction)
    residual = residual - step_next * (applied_residual + ratio * applied)
    return (solution, residual)


def solution(mesh):
    placed = (
        P(None, ("band", "lon"), None),
        P(("band", "lon"), None),
        P(None, ("band", "lon"), None),
        P(("band", "lon"), None, None),
        P(("band", "lon"), None, None, None),
        P(("band", "lon"), None, None),
        P(("band", "lon"), None, None, None),
        P(("band", "lon"), None),
        P(("band", "lon"), None),
        P(("band", "lon"), None),
        P(("band", "lon")),
    )
    return jax.shard_map(
        on_device,
        mesh=mesh,
        in_specs=placed,
        out_specs=(P(None, ("band", "lon"), None), P(None, ("band", "lon"), None)),
        check_vma=False,
    )
```

```python
import math

import jax
import jax.numpy as jnp
from jax import lax
from jax.sharding import PartitionSpec as P

REACH = 6
ITERS = 2


MATMUL_PRECISION = lax.Precision.HIGH
ROOT_THREE = math.sqrt(3.0)
AMPLITUDE = 0.02


def extended(cells, sides, width):
    for axis, dim in sides:
        count = lax.axis_size(axis)
        head = lax.slice_in_dim(cells, 0, width, axis=dim)
        tail = lax.slice_in_dim(cells, cells.shape[dim] - width, cells.shape[dim], axis=dim)
        cells = jnp.concatenate(
            [
                lax.ppermute(tail, axis, [(i, (i + 1) % count) for i in range(count)]),
                cells,
                lax.ppermute(head, axis, [((i + 1) % count, i) for i in range(count)]),
            ],
            axis=dim,
        )
    return cells


def gathered(vector, axis):
    count = lax.axis_size(axis)
    copies = jnp.broadcast_to(vector[None], (count,) + vector.shape)
    return lax.all_to_all(copies, axis, 0, 0, tiled=False)


def all_sum(vector, axes):
    for axis in axes:
        vector = jnp.sum(gathered(vector, axis), axis=0)
    return vector


def matern_shape(rows_pos, cols_pos, length_scale):
    squared = None
    for component in range(3):
        offset = rows_pos[component][:, :, None] - cols_pos[component][:, None, :]
        squared = offset * offset if squared is None else squared + offset * offset
    scaled = jnp.sqrt(squared) * (ROOT_THREE / length_scale)
    return (1.0 + scaled) * jnp.exp(-scaled)


def on_device(
    sky_maps,
    noise_var,
    position,
    leaf_basis,
    leaf_couple,
    transfer,
    panel_couple,
    near_list,
    far_list,
    panel_list,
    leaf_panel,
):
    lon_index = lax.axis_index("lon")
    lon_count = lax.axis_size("lon")
    local_leaves = sky_maps.shape[1]
    pixel_count = sky_maps.shape[2]
    cycle_size = local_leaves * lon_count
    panel_count = panel_couple.shape[0]
    length_scale = 2.0 * math.pi / cycle_size
    first_leaf = lon_index * local_leaves
    near_depth = 2

    def rim_index(leaf_ids, depth):
        return (leaf_ids % cycle_size - first_leaf + depth) % cycle_size

    near_valid = near_list >= 0
    near_rows = rim_index(jnp.where(near_valid, near_list, near_list[:, :1]), near_depth)
    far_rows = rim_index(far_list, REACH)
    rim_pos = extended(position, (("lon", 1),), near_depth)

    same_blocks = matern_shape(
        rim_pos[:, near_depth : near_depth + local_leaves],
        rim_pos[:, near_depth : near_depth + local_leaves],
        length_scale,
    )
    step_blocks = [
        matern_shape(
            rim_pos[:, near_depth - step : near_depth + local_leaves],
            rim_pos[:, near_depth : near_depth + local_leaves + step],
            length_scale,
        )
        for step in range(1, near_depth + 1)
    ]
    step_range = jnp.arange(-near_depth, near_depth + 1, dtype=jnp.int32)
    targets = jnp.arange(local_leaves, dtype=jnp.int32)[:, None] + near_depth + step_range[None, :]
    matches = (near_rows[:, :, None] == targets[:, None, :]) & near_valid[:, :, None]
    offset_scale = AMPLITUDE * jnp.sum(matches.astype(jnp.float32), axis=1)
    band_slot = panel_list // (lon_count * panel_count)
    gathered_rows = band_slot * panel_count + panel_list % panel_count
    membership = (leaf_panel[:, None] == jnp.arange(panel_count, dtype=jnp.int32)[None, :]).astype(
        jnp.float32
    )

    far_steps = [step for step in range(-REACH, REACH + 1) if abs(step) >= 3]
    far_pick = [
        (far_rows == jnp.arange(local_leaves, dtype=jnp.int32)[:, None] + REACH + step).astype(
            jnp.float32
        )
        for step in far_steps
    ]

    def far_coeffs(rim_coeffs):
        picked = None
        for step, pick in zip(far_steps, far_pick):
            near_slice = rim_coeffs[:, REACH + step : REACH + step + local_leaves]
            term = pick[None, :, :, None] * near_slice[:, :, None, :]
            picked = term if picked is None else picked + term
        return picked

    def covariance_local(direction):
        coeffs = jnp.einsum("lpr,mlp->mlr", leaf_basis, direction, precision=MATMUL_PRECISION)
        joined = jnp.concatenate([direction, coeffs], axis=2)
        rim_joined = extended(joined, (("lon", 1),), REACH)
        rim_values = rim_joined[
            :, REACH - near_depth : REACH + local_leaves + near_depth, :pixel_count
        ]
        rim_coeffs = rim_joined[:, :, pixel_count:]

        def offset_values(step):
            start = near_depth + step
            values = rim_values[:, start : start + local_leaves]
            return values * offset_scale[None, :, step + near_depth, None]

        near_part = jnp.einsum(
            "ipq,miq->mip", same_blocks, offset_values(0), precision=MATMUL_PRECISION
        )
        for step in range(1, near_depth + 1):
            blocks = step_blocks[step - 1]
            ahead = blocks[step : step + local_leaves]
            behind = blocks[:local_leaves]
            near_part = near_part + jnp.einsum(
                "ipq,miq->mip", ahead, offset_values(step), precision=MATMUL_PRECISION
            )
            near_part = near_part + jnp.einsum(
                "iqp,miq->mip", behind, offset_values(-step), precision=MATMUL_PRECISION
            )
        leaf_far = jnp.einsum(
            "lsab,mlsb->mla", leaf_couple, far_coeffs(rim_coeffs), precision=MATMUL_PRECISION
        )
        upward = jnp.einsum("lab,mla->mlb", transfer, coeffs, precision=MATMUL_PRECISION)
        panel_coeffs = jnp.sum(membership[None, :, :, None] * upward[:, :, None, :], axis=1)
        return direction, near_part, leaf_far, panel_coeffs

    def band_layout(band_panels, panel_coeffs):
        stacked = band_panels.reshape((band_panels.shape[0],) + panel_coeffs.shape)
        return jnp.swapaxes(stacked, 0, 1).reshape(
            panel_coeffs.shape[0], -1, panel_coeffs.shape[2]
        )

    def covariance_finish(local, band_coeffs):
        direction, near_part, leaf_far, panel_coeffs = local
        panel_far = jnp.einsum(
            "ksab,mksb->mka",
            panel_couple,
            band_coeffs[:, gathered_rows],
            precision=MATMUL_PRECISION,
        )
        downward = jnp.sum(membership[None, :, :, None] * panel_far[:, None, :, :], axis=2)
        leaf_far = leaf_far + jnp.einsum(
            "lab,mlb->mla", transfer, downward, precision=MATMUL_PRECISION
        )
        far_part = jnp.einsum("lpr,mlr->mlp", leaf_basis, leaf_far, precision=MATMUL_PRECISION)
        return noise_var[None] * direction + near_part + far_part

    def covariance_apply(direction):
        local = covariance_local(direction)
        panel_coeffs = local[3]
        band_panels = gathered(panel_coeffs.reshape(-1), "band")
        return covariance_finish(local, band_layout(band_panels, panel_coeffs))

    def total(*products):
        sums = jnp.stack([jnp.sum(product, axis=(1, 2)) for product in products])
        return all_sum(sums, ("lon", "band"))

    assert ITERS == 2
    direction = sky_maps
    applied = covariance_apply(direction)
    applied_local = covariance_local(applied)
    first_sums = jnp.stack(
        [jnp.sum(product, axis=(1, 2)) for product in (direction * direction, direction * applied)]
    )
    first_sums = all_sum(first_sums, ("lon",))
    panel_coeffs = applied_local[3]
    payload = jnp.concatenate([panel_coeffs.reshape(-1), first_sums.reshape(-1)])
    band_payload = gathered(payload, "band")
    panel_size = panel_coeffs.size
    norm_now, curvature_sum = jnp.sum(band_payload[:, panel_size:], axis=0).reshape(
        first_sums.shape
    )
    applied_twice = covariance_finish(
        applied_local, band_layout(band_payload[:, :panel_size], panel_coeffs)
    )
    step_size = (norm_now / curvature_sum)[:, None, None]
    solution = step_size * direction
    residual = direction - step_size * applied
    applied_residual = applied - step_size * applied_twice
    norm_next, residual_curv, cross_one, cross_two = total(
        residual * residual,
        residual * applied_residual,
        residual * applied,
        direction * applied_residual,
    )
    ratio = norm_next / norm_now
    next_curv = residual_curv + ratio * (cross_one + cross_two) + ratio * ratio * curvature_sum
    ratio = ratio[:, None, None]
    step_next = (norm_next / next_curv)[:, None, None]
    solution = solution + step_next * (residual + ratio * direction)
    residual = residual - step_next * (applied_residual + ratio * applied)
    return (solution, residual)


def solution(mesh):
    placed = (
        P(None, ("band", "lon"), None),
        P(("band", "lon"), None),
        P(None, ("band", "lon"), None),
        P(("band", "lon"), None, None),
        P(("band", "lon"), None, None, None),
        P(("band", "lon"), None, None),
        P(("band", "lon"), None, None, None),
        P(("band", "lon"), None),
        P(("band", "lon"), None),
        P(("band", "lon"), None),
        P(("band", "lon")),
    )
    return jax.shard_map(
        on_device,
        mesh=mesh,
        in_specs=placed,
        out_specs=(P(None, ("band", "lon"), None), P(None, ("band", "lon"), None)),
        check_vma=False,
    )
```
